128 devices in a mesh: mem: 8 (over x, core), tile: 16 (over y, z).
Axes of the slice: x: 4, y: 4, z: 4, core: 2. Of those that a mesh axis runs over, the one named last changes fastest.
Arguments:
- background: bfloat16 [512, 8, 16, 1024], P('mem', None, 'tile'), may hold values from -6 to 6
- evolved: bfloat16 [512, 131072], P('mem', 'tile'), may hold values from -6 to 6
- obs_value: bfloat16 [131072], P('tile'), may hold values from -8 to 8
- obs_var: bfloat16 [131072], P('tile'), may hold values from 0.5 to 2
- obs_patch: int32 [131072, 1], P('tile'), may hold values from 0 to 127; in each aligned block of 8192 rows (0 to 8191, 8192 to 16383, ...) at most 128 rows name the same one
- obs_pos: int32 [131072], P('tile'), may hold values from 0 to 127
Outputs:
- analysis: bfloat16 [512, 8, 16, 1024], P('mem', None, 'tile')
The draws below stay inside these ranges and needn't reach their ends.
Inputs may be any that keep to these rules, and one draw needn't show every extreme that they name: `obs_patch`: in each aligned block of 8192 rows (the observations of one tile index) no patch is named by more than 128 rows, a bound that some block reaches.
All inputs are finite; a program needn't handle non-finite values.
Results may differ from the reference program's by a relative error of at most 0.0065.
Values may be sent and summed in bfloat16 or wider, within the bound.
No kernel may reach another device: no remote copies, remote signals or barrier semaphores. Data moves between devices by JAX's collectives and lax.ppermute only.
A program may use at most 64 MiB of HBM per device.

```python
import math
import jax
import jax.numpy as jnp
import numpy as np
from jax import lax

MEMBERS = 512
PATCH_CELLS = 128
ITERS = 4
PATCHES = 128
CELLS = 1024
SLOTS = 2048
CAPACITY = 128
OBS_DEV = 8192
OBS_ALL = 131072
N_MEM = 8
N_TILE = 16


def plant(values, key, least, high):
    longest = values.shape.index(max(values.shape))
    spots = []
    for shift in (0, 1):
        where = [jax.random.randint(jax.random.fold_in(key, axis), (), 0, length) for axis, length in enumerate(values.shape)]
        where[longest] = (where[longest] + shift) % values.shape[longest]
        spots.append(tuple(where))
    return values.at[spots[0]].set(least).at[spots[1]].set(high)


def levels(key, dims, split, low, largest):
    def one(axis_at, parts):
        heights = jax.random.uniform(jax.random.fold_in(jax.random.fold_in(key, 6), axis_at), (parts,), jnp.float32, low / len(split), largest / len(split))
        return jnp.repeat(jnp.exp(heights), dims[axis_at] // parts).reshape((-1,) + (1,) * (len(dims) - axis_at - 1))

    level = one(*split[0])
    for cut in split[1:]:
        level = level * one(*cut)
    return level


def routed_block(stream_key, own, number, rows, amount, top, reach, slope):
    order = jax.random.permutation(stream_key, amount)
    packed, usual = load_shares(amount, rows * top, reach, slope, True), load_shares(amount, rows * top, reach, slope, False)
    places = jnp.arange(amount)

    def named(tallies, turn):
        used = int((tallies > 0).sum())
        fixed = max(1, used // 4)
        moved = fixed + (places - fixed + turn * (used - fixed)) % max(1, amount - fixed)
        return jnp.zeros((amount,), jnp.int32).at[order[jnp.where(places < fixed, places, moved)]].set(jnp.asarray(tallies, jnp.int32))

    tallies = jnp.where(number % 4 == 0, named(packed, number // 4), named(usual, number - number // 4 - 1))
    mixed = jax.random.permutation(jax.random.fold_in(own, 3), amount)
    giver, taker = mixed[0:amount // 2 * 2:2], mixed[1:amount // 2 * 2:2]
    slack = jnp.minimum(tallies[giver] - 1, reach - tallies[taker]) // 2
    slack = jnp.where((giver == order[0]) | (taker == order[0]) | (tallies[taker] == 0), 0, jnp.maximum(slack, 0))
    moved = jax.random.randint(jax.random.fold_in(own, 4), (amount // 2,), 0, 1 << 20) % (slack + 1)
    tallies = tallies.at[giver].add(-moved).at[taker].add(moved)
    items = jnp.searchsorted(jnp.cumsum(tallies), jnp.arange(rows * top), side="right").astype(jnp.int32)
    listing = items.reshape(top, rows).T
    listing = listing[jax.random.permutation(jax.random.fold_in(own, 1), rows)]
    turn = jax.random.randint(jax.random.fold_in(own, 2), (rows, 1), 0, top)
    return jnp.take_along_axis(listing, (jnp.arange(top)[None, :] + turn) % top, axis=1)


def load_shares(number_of, total, limit, slope, full):
    portions = [(1 << 20) // math.isqrt(standing ** slope) + 1 for standing in range(1, number_of + 1)]
    largest = limit if full else min(limit, max(-(-total // number_of), total * portions[0] // sum(portions)))
    least = 1 if total - largest >= number_of - 1 else 0
    given, spare = [largest] + [least] * (number_of - 1), total - largest - least * (number_of - 1)
    while spare > 0:
        candidates = [i for i in range(1, number_of) if given[i] < largest] or [i for i in range(1, number_of) if given[i] < limit]
        mass, budget = sum([portions[i] for i in candidates]), spare
        for i in candidates:
            more = min(limit - given[i], max(1, budget * portions[i] // mass), spare)
            given[i] = given[i] + more
            spare = spare - more
    return np.array(given)


def normal_values(stream_key, shape, scale, most, cuts=(), kind=jnp.bfloat16):
    factor_of = levels(stream_key, shape, cuts, -0.22, 0.18) if cuts else 1.0
    values = jax.random.normal(stream_key, shape, jnp.float32) * scale * factor_of
    return jnp.minimum(jnp.maximum(values, -most), most).astype(kind)


def setup_inputs(seed: int = 0) -> dict:
    key_list = jax.random.split(jax.random.key(seed), 7)
    background = normal_values(key_list[0], (MEMBERS, N_MEM, N_TILE, CELLS), 1.0, 6.0, ((0, 8), (2, 16)))
    evolved = normal_values(key_list[1], (MEMBERS, OBS_ALL), 1.0, 6.0, ((0, 8), (1, 16)))
    obs_value = normal_values(key_list[2], (OBS_ALL,), 1.5, 8.0, ((0, 16),))
    obs_var = jnp.clip(jnp.exp(math.log(2.0) - 1.3862944 * jax.random.uniform(key_list[3], (OBS_ALL,), jnp.float32) ** levels(key_list[3], (OBS_ALL,), ((0, 16),), -0.2, 0.2)), 0.5, 2.0).astype(jnp.bfloat16)
    obs_patch_keys = jax.random.split(jax.random.fold_in(key_list[4], 1), OBS_ALL // OBS_DEV)
    obs_patch_turns = jax.random.permutation(jax.random.fold_in(key_list[4], 3), OBS_ALL // OBS_DEV)
    obs_patch = jax.vmap(lambda own, number: routed_block(jax.random.fold_in(key_list[4], 2), own, number, OBS_DEV, PATCHES, 1, CAPACITY, 2))(obs_patch_keys, obs_patch_turns).reshape((OBS_ALL, 1))
    obs_pos = plant(jax.random.randint(key_list[5], (OBS_ALL,), 0, PATCH_CELLS), jax.random.fold_in(key_list[5], 1), 0, PATCH_CELLS - 1).astype(jnp.int32)
    return dict(background=background, evolved=evolved, obs_value=obs_value, obs_var=obs_var, obs_patch=obs_patch, obs_pos=obs_pos)


def localize(position, offset):
    distance = (offset * PATCH_CELLS + position + 0.5 - 0.5 * PATCH_CELLS) / PATCH_CELLS
    return jnp.exp(-2.0 * distance * distance)

def gram_terms(centred, innovation, weight, loc_weight):
    weighted = (centred.astype(jnp.float32) * (weight * loc_weight)[None, :]).astype(jnp.bfloat16)
    gram_mat = lax.dot_general(weighted, centred, (((1,), (1,)), ((), ())), preferred_element_type=jnp.float32)
    gram_vec = jnp.dot(weighted, innovation, preferred_element_type=jnp.float32)
    return (gram_mat, gram_vec)

def inverse_root(gram_mat):
    mat_size = gram_mat.shape[0]
    identity = jnp.eye(mat_size, dtype=jnp.float32)
    norm_scale = jnp.sqrt(jnp.sum(gram_mat * gram_mat))
    root_up = gram_mat / norm_scale
    root_down = identity
    for sweep_index in range(ITERS):
        middle = 1.5 * identity - 0.5 * jnp.dot(root_down, root_up, precision=lax.Precision.HIGHEST)
        root_up = jnp.dot(root_up, middle, precision=lax.Precision.HIGHEST)
        root_down = jnp.dot(middle, root_down, precision=lax.Precision.HIGHEST)
    return root_down / jnp.sqrt(norm_scale)

def transform(gram_mat, gram_vec):
    mat_size = gram_mat.shape[0]
    identity = jnp.eye(mat_size, dtype=jnp.float32)
    inv_root = inverse_root(gram_mat + (mat_size - 1.0) * identity)
    inner_w = jnp.dot(inv_root, gram_vec, precision=lax.Precision.HIGHEST)
    mean_w = jnp.dot(inv_root, inner_w, precision=lax.Precision.HIGHEST)
    return (math.sqrt(mat_size - 1.0) * inv_root + mean_w[:, None]).astype(jnp.bfloat16)

def update(states, transform_mat):
    members = states.shape[0]
    state_mean = lax.optimization_barrier(jnp.sum(states.astype(jnp.float32), 0)) / members
    deviation = (states.astype(jnp.float32) - state_mean[None, :]).astype(jnp.bfloat16)
    mixed = lax.dot_general(transform_mat, deviation, (((0,), (0,)), ((), ())), preferred_element_type=jnp.float32)
    return (state_mean[None, :] + mixed).astype(jnp.bfloat16)

def reference(background, evolved, obs_value, obs_var, obs_patch, obs_pos):
    obs_total = evolved.shape[1]
    target = obs_patch[:, 0]
    obs_mean = lax.optimization_barrier(jnp.sum(evolved.astype(jnp.float32), 0)) / MEMBERS
    centred = (evolved.astype(jnp.float32) - obs_mean[None, :]).astype(jnp.bfloat16)
    innovation = (obs_value.astype(jnp.float32) - obs_mean).astype(jnp.bfloat16)
    weight = 1.0 / obs_var.astype(jnp.float32)
    onehot = (target[:, None] == jnp.arange(PATCHES, dtype=jnp.int32)[None, :]).astype(jnp.int32)
    slot_rank = lax.optimization_barrier(jnp.sum(jnp.cumsum(onehot, 0) * onehot, 1)) - 1
    slot_place = (target * SLOTS + slot_rank).astype(jnp.int32)
    table = jnp.full((PATCHES * SLOTS,), obs_total, jnp.int32)
    table = table.at[slot_place].set(jnp.arange(obs_total, dtype=jnp.int32)).reshape(PATCHES, SLOTS)
    centred_pad = jnp.concatenate([centred, jnp.zeros((MEMBERS, 1), jnp.bfloat16)], 1)
    innovation_pad = jnp.concatenate([innovation, jnp.zeros((1,), jnp.bfloat16)])
    weight_pad = jnp.concatenate([weight, jnp.zeros((1,), jnp.float32)])
    position_pad = jnp.concatenate([obs_pos.astype(jnp.float32), jnp.zeros((1,), jnp.float32)])
    offset = jnp.repeat(jnp.array([-1.0, 0.0, 1.0], jnp.float32), SLOTS)

    def one_patch(patch_index):
        below = (patch_index + PATCHES - 1) % PATCHES
        above = (patch_index + 1) % PATCHES
        slot_rows = jnp.concatenate([table[below], table[patch_index], table[above]])
        gram_mat, gram_vec = gram_terms(centred_pad[:, slot_rows], innovation_pad[slot_rows], weight_pad[slot_rows], localize(position_pad[slot_rows], offset))
        transform_mat = transform(gram_mat, gram_vec)
        states = background[:, patch_index // N_TILE, patch_index % N_TILE, :]
        return update(states, transform_mat)
    result = lax.map(one_patch, jnp.arange(PATCHES, dtype=jnp.int32))
    return result.reshape(N_MEM, N_TILE, MEMBERS, CELLS).transpose(2, 0, 1, 3)
```

```python
import math

import jax
import jax.numpy as jnp
from jax import lax
from jax.sharding import PartitionSpec as P

PATCH_CELLS = 128
OBS_PATCH = 1024
ITERS = 4
HIGHEST = lax.Precision.HIGHEST


def ring_shift(block, axis, step):
    count = 1
    for name in axis:
        count *= lax.axis_size(name)
    pairs = [(i, (i + step) % count) for i in range(count)]
    return lax.ppermute(block, axis, pairs)


def localize(position, offset):
    distance = (offset * PATCH_CELLS + position + 0.5 - 0.5 * PATCH_CELLS) / PATCH_CELLS
    return jnp.exp(-2.0 * distance * distance)


def obs_weight(var_row, shifted_row):
    is_live = shifted_row.astype(jnp.float32) > 0.5
    safe_var = jnp.where(is_live, var_row.astype(jnp.float32), 1.0)
    return (jnp.where(is_live, 1.0 / safe_var, 0.0), shifted_row.astype(jnp.float32) - 1.0)


def block_terms(block, members, offset):
    centred = block[:members]
    innovation = block[members]
    weight, position = obs_weight(block[members + 1], block[members + 2])
    scale = weight * localize(position, offset)
    weighted = (centred.astype(jnp.float32) * scale[None, :]).astype(jnp.bfloat16)
    gram_mat = lax.dot_general(
        weighted, centred, (((1,), (1,)), ((), ())), preferred_element_type=jnp.float32
    )
    gram_vec = jnp.dot(weighted, innovation, preferred_element_type=jnp.float32)
    return gram_mat, gram_vec


def inverse_root(gram_mat):
    mat_size = gram_mat.shape[0]
    identity = jnp.eye(mat_size, dtype=jnp.float32)
    norm_scale = jnp.sqrt(jnp.sum(gram_mat * gram_mat))
    root_up = gram_mat / norm_scale
    root_down = None
    for sweep_index in range(ITERS):
        if root_down is None:
            product = root_up
        else:
            product = jnp.dot(root_down, root_up, precision=HIGHEST)
        middle = 1.5 * identity - 0.5 * product
        if sweep_index + 1 < ITERS:
            root_up = jnp.dot(root_up, middle, precision=HIGHEST)
        root_down = middle if root_down is None else jnp.dot(middle, root_down, precision=HIGHEST)
    return root_down / jnp.sqrt(norm_scale)


def transform(gram_mat, gram_vec):
    mat_size = gram_mat.shape[0]
    identity = jnp.eye(mat_size, dtype=jnp.float32)
    inv_root = inverse_root(gram_mat + (mat_size - 1.0) * identity)
    inner_w = jnp.dot(inv_root, gram_vec, precision=HIGHEST)
    mean_w = jnp.dot(inv_root, inner_w, precision=HIGHEST)
    return (math.sqrt(mat_size - 1.0) * inv_root + mean_w[:, None]).astype(jnp.bfloat16)


def per_device(background, evolved, obs_value, obs_var, obs_patch, obs_pos):
    mem_count = lax.axis_size("mem")
    tile_count = lax.axis_size("tile")
    patches = mem_count * tile_count
    local_members = evolved.shape[0]
    members = local_members * mem_count
    slot_count = 2 * OBS_PATCH
    capacity = slot_count // tile_count
    cells = background.shape[3]

    states = lax.all_to_all(background, "mem", split_axis=1, concat_axis=0, tiled=True)
    flat_states = states.reshape(members, cells)
    state_sum = jnp.sum(flat_states.astype(jnp.float32), 0)
    state_mean = state_sum / members
    deviation = (flat_states.astype(jnp.float32) - state_mean[None, :]).astype(jnp.bfloat16)

    target = obs_patch[:, 0]
    onehot = (target[:, None] == jnp.arange(patches, dtype=jnp.int32)[None, :]).astype(jnp.int32)
    slot_rank = jnp.sum(jnp.cumsum(onehot, 0) * onehot, 1) - 1
    slot_place = target * capacity + slot_rank
    rows = jnp.concatenate(
        [evolved, jnp.stack([obs_value, obs_var, (obs_pos + 1).astype(jnp.bfloat16)])], 0
    )
    send = jnp.zeros((rows.shape[0], patches * capacity), jnp.bfloat16).at[:, slot_place].set(rows)
    got = lax.all_to_all(send, ("mem", "tile"), split_axis=1, concat_axis=1, tiled=True)
    got = got.reshape(rows.shape[0], mem_count, slot_count)
    gathered = got[:local_members].transpose(1, 0, 2).reshape(members, slot_count)
    got_info = got[local_members:, 0]

    obs_mean = jnp.sum(gathered.astype(jnp.float32), 0) / members
    centred = (gathered.astype(jnp.float32) - obs_mean[None, :]).astype(jnp.bfloat16)
    innovation = (got_info[0].astype(jnp.float32) - obs_mean).astype(jnp.bfloat16)
    stacked = jnp.concatenate([centred, innovation[None, :], got_info[1:3]], 0)
    axis = ("mem", "tile")
    low = ring_shift(stacked, axis, 1)
    high = ring_shift(stacked, axis, -1)

    gram_mat, gram_vec = block_terms(stacked, members, 0.0)
    for block, offset in ((low, -1.0), (high, 1.0)):
        more_mat, more_vec = block_terms(block, members, offset)
        gram_mat = gram_mat + more_mat
        gram_vec = gram_vec + more_vec
    transform_mat = transform(gram_mat, gram_vec)

    mixed = lax.dot_general(
        transform_mat, deviation, (((0,), (0,)), ((), ())), preferred_element_type=jnp.float32
    )
    updated = (state_mean[None, :] + mixed).astype(jnp.bfloat16)
    back = lax.all_to_all(
        updated.reshape(mem_count, local_members, cells), "mem", split_axis=0, concat_axis=0, tiled=True
    )
    return back.transpose(1, 0, 2).reshape(local_members, mem_count, 1, cells)


def solution(mesh):
    return jax.shard_map(
        per_device,
        mesh=mesh,
        in_specs=(
            P("mem", None, "tile", None),
            P("mem", "tile"),
            P("tile"),
            P("tile"),
            P("tile", None),
            P("tile"),
        ),
        out_specs=P("mem", None, "tile", None),
        check_vma=False,
    )
```

```python
import math

import jax
import jax.numpy as jnp
from jax import lax
from jax.sharding import PartitionSpec as P

PATCH_CELLS = 128
OBS_PATCH = 1024
ITERS = 4
HIGHEST = lax.Precision.HIGHEST


def ring_shift(block, axis, step):
    count = 1
    for name in axis:
        count *= lax.axis_size(name)
    pairs = [(i, (i + step) % count) for i in range(count)]
    return lax.ppermute(block, axis, pairs)


def localize(position, offset):
    distance = (offset * PATCH_CELLS + position + 0.5 - 0.5 * PATCH_CELLS) / PATCH_CELLS
    return jnp.exp(-2.0 * distance * distance)


def obs_weight(var_row, shifted_row):
    is_live = shifted_row.astype(jnp.float32) > 0.5
    safe_var = jnp.where(is_live, var_row.astype(jnp.float32), 1.0)
    return (jnp.where(is_live, 1.0 / safe_var, 0.0), shifted_row.astype(jnp.float32) - 1.0)


def block_terms(block, members, offset):
    centred = block[:members]
    innovation = block[members]
    weight, position = obs_weight(block[members + 1], block[members + 2])
    scale = weight * localize(position, offset)
    weighted = (centred.astype(jnp.float32) * scale[None, :]).astype(jnp.bfloat16)
    gram_mat = lax.dot_general(
        weighted, centred, (((1,), (1,)), ((), ())), preferred_element_type=jnp.float32
    )
    gram_vec = jnp.dot(weighted, innovation, preferred_element_type=jnp.float32)
    return gram_mat, gram_vec


def inverse_root(gram_mat):
    mat_size = gram_mat.shape[0]
    identity = jnp.eye(mat_size, dtype=jnp.float32)
    norm_scale = jnp.sqrt(jnp.sum(gram_mat * gram_mat))
    root_up = gram_mat / norm_scale
    root_down = None
    for sweep_index in range(ITERS):
        if root_down is None:
            product = root_up
        else:
            product = jnp.dot(root_down, root_up, precision=HIGHEST)
        middle = 1.5 * identity - 0.5 * product
        if sweep_index + 1 < ITERS:
            root_up = jnp.dot(root_up, middle, precision=HIGHEST)
        root_down = middle if root_down is None else jnp.dot(middle, root_down, precision=HIGHEST)
    return root_down / jnp.sqrt(norm_scale)


def transform(gram_mat, gram_vec):
    mat_size = gram_mat.shape[0]
    identity = jnp.eye(mat_size, dtype=jnp.float32)
    inv_root = inverse_root(gram_mat + (mat_size - 1.0) * identity)
    inner_w = jnp.dot(inv_root, gram_vec, precision=HIGHEST)
    mean_w = jnp.dot(inv_root, inner_w, precision=HIGHEST)
    return (math.sqrt(mat_size - 1.0) * inv_root + mean_w[:, None]).astype(jnp.bfloat16)


def per_device(background, evolved, obs_value, obs_var, obs_patch, obs_pos):
    mem_count = lax.axis_size("mem")
    tile_count = lax.axis_size("tile")
    patches = mem_count * tile_count
    local_members = evolved.shape[0]
    members = local_members * mem_count
    slot_count = 2 * OBS_PATCH
    capacity = slot_count // tile_count
    cells = background.shape[3]

    states = lax.all_to_all(background, "mem", split_axis=1, concat_axis=0, tiled=True)
    flat_states = states.reshape(members, cells)
    state_sum = jnp.sum(flat_states.astype(jnp.float32), 0)
    state_mean = state_sum / members
    deviation = (flat_states.astype(jnp.float32) - state_mean[None, :]).astype(jnp.bfloat16)

    target = obs_patch[:, 0]
    onehot = (target[:, None] == jnp.arange(patches, dtype=jnp.int32)[None, :]).astype(jnp.int32)
    slot_rank = jnp.sum(jnp.cumsum(onehot, 0) * onehot, 1) - 1
    slot_place = target * capacity + slot_rank
    rows = jnp.concatenate(
        [evolved, jnp.stack([obs_value, obs_var, (obs_pos + 1).astype(jnp.bfloat16)])], 0
    )
    send = jnp.zeros((rows.shape[0], patches * capacity), jnp.bfloat16).at[:, slot_place].set(rows)
    got = lax.all_to_all(send, ("mem", "tile"), split_axis=1, concat_axis=1, tiled=True)
    got = got.reshape(rows.shape[0], mem_count, slot_count)
    gathered = got[:local_members].transpose(1, 0, 2).reshape(members, slot_count)
    got_info = got[local_members:, 0]

    obs_mean = jnp.sum(gathered.astype(jnp.float32), 0) / members
    centred = (gathered.astype(jnp.float32) - obs_mean[None, :]).astype(jnp.bfloat16)
    innovation = (got_info[0].astype(jnp.float32) - obs_mean).astype(jnp.bfloat16)
    stacked = jnp.concatenate([centred, innovation[None, :], got_info[1:3]], 0)
    axis = ("mem", "tile")
    next_mat, next_vec = block_terms(stacked, members, -1.0)
    prev_mat, prev_vec = block_terms(stacked, members, 1.0)
    from_prev = ring_shift(next_mat, axis, 1)
    from_prev_vec = ring_shift(next_vec, axis, 1)
    from_next = ring_shift(prev_mat, axis, -1)
    from_next_vec = ring_shift(prev_vec, axis, -1)
    own_mat, own_vec = block_terms(stacked, members, 0.0)
    gram_mat = own_mat + from_prev + from_next
    gram_vec = own_vec + from_prev_vec + from_next_vec
    transform_mat = transform(gram_mat, gram_vec)

    mixed = lax.dot_general(
        transform_mat, deviation, (((0,), (0,)), ((), ())), preferred_element_type=jnp.float32
    )
    updated = (state_mean[None, :] + mixed).astype(jnp.bfloat16)
    chunks = updated.reshape(mem_count, local_members, cells)
    me = lax.axis_index("mem")
    pieces = []
    for shift in range(mem_count):
        piece = lax.dynamic_index_in_dim(chunks, (me + shift) % mem_count, 0, keepdims=False)
        if shift:
            pairs = [(i, (i + shift) % mem_count) for i in range(mem_count)]
            piece = lax.ppermute(piece, "mem", pairs)
        pieces.append(piece)
    by_shift = jnp.stack(pieces)
    back = jnp.take(by_shift, (me - jnp.arange(mem_count)) % mem_count, axis=0)
    return back.transpose(1, 0, 2).reshape(local_members, mem_count, 1, cells)


def solution(mesh):
    return jax.shard_map(
        per_device,
        mesh=mesh,
        in_specs=(
            P("mem", None, "tile", None),
            P("mem", "tile"),
            P("tile"),
            P("tile"),
            P("tile", None),
            P("tile"),
        ),
        out_specs=P("mem", None, "tile", None),
        check_vma=False,
    )
```

```python
import math

import jax
import jax.numpy as jnp
from jax import lax
from jax.sharding import PartitionSpec as P

PATCH_CELLS = 128
OBS_PATCH = 1024
ITERS = 4
HIGHEST = lax.Precision.HIGHEST
NEWTON = lax.Precision.HIGH


def ring_shift(block, axis, step):
    count = 1
    for name in axis:
        count *= lax.axis_size(name)
    pairs = [(i, (i + step) % count) for i in range(count)]
    return lax.ppermute(block, axis, pairs)


def localize(position, offset):
    distance = (offset * PATCH_CELLS + position + 0.5 - 0.5 * PATCH_CELLS) / PATCH_CELLS
    return jnp.exp(-2.0 * distance * distance)


def obs_weight(var_row, shifted_row):
    is_live = shifted_row.astype(jnp.float32) > 0.5
    safe_var = jnp.where(is_live, var_row.astype(jnp.float32), 1.0)
    return (jnp.where(is_live, 1.0 / safe_var, 0.0), shifted_row.astype(jnp.float32) - 1.0)


def block_terms(block, members, offset):
    centred = block[:members]
    innovation = block[members]
    weight, position = obs_weight(block[members + 1], block[members + 2])
    scale = weight * localize(position, offset)
    weighted = (centred.astype(jnp.float32) * scale[None, :]).astype(jnp.bfloat16)
    gram_mat = lax.dot_general(
        weighted, centred, (((1,), (1,)), ((), ())), preferred_element_type=jnp.float32
    )
    gram_vec = jnp.dot(weighted, innovation, preferred_element_type=jnp.float32)
    return gram_mat, gram_vec


def inverse_root(gram_mat):
    mat_size = gram_mat.shape[0]
    identity = jnp.eye(mat_size, dtype=jnp.float32)
    norm_scale = jnp.sqrt(jnp.sum(gram_mat * gram_mat))
    root_up = gram_mat / norm_scale
    root_down = None
    for sweep_index in range(ITERS):
        if root_down is None:
            product = root_up
        else:
            product = jnp.dot(root_down, root_up, precision=NEWTON)
        middle = 1.5 * identity - 0.5 * product
        if sweep_index + 1 < ITERS:
            root_up = jnp.dot(root_up, middle, precision=NEWTON)
        root_down = middle if root_down is None else jnp.dot(middle, root_down, precision=NEWTON)
    return root_down / jnp.sqrt(norm_scale)


def transform(gram_mat, gram_vec):
    mat_size = gram_mat.shape[0]
    identity = jnp.eye(mat_size, dtype=jnp.float32)
    inv_root = inverse_root(gram_mat + (mat_size - 1.0) * identity)
    inner_w = jnp.dot(inv_root, gram_vec, precision=HIGHEST)
    mean_w = jnp.dot(inv_root, inner_w, precision=HIGHEST)
    return (math.sqrt(mat_size - 1.0) * inv_root + mean_w[:, None]).astype(jnp.bfloat16)


def rank_in_patch(target, patches):
    rows = target.shape[0]
    block = 128
    blocks = rows // block
    onehot = (target[:, None] == jnp.arange(patches, dtype=jnp.int32)[None, :]).astype(jnp.bfloat16)
    onehot = onehot.reshape(blocks, block, patches)
    lower = (jnp.arange(block)[:, None] >= jnp.arange(block)[None, :]).astype(jnp.bfloat16)
    within = jnp.einsum("ij,bjp->bip", lower, onehot, preferred_element_type=jnp.float32)
    totals = jnp.sum(onehot.astype(jnp.float32), 1)
    earlier = (jnp.arange(blocks)[:, None] > jnp.arange(blocks)[None, :]).astype(jnp.float32)
    before = jnp.dot(earlier, totals, precision=HIGHEST)
    count = jnp.sum((within + before[:, None, :]) * onehot.astype(jnp.float32), 2)
    return count.reshape(rows).astype(jnp.int32) - 1


def per_device(background, evolved, obs_value, obs_var, obs_patch, obs_pos):
    mem_count = lax.axis_size("mem")
    tile_count = lax.axis_size("tile")
    patches = mem_count * tile_count
    local_members = evolved.shape[0]
    members = local_members * mem_count
    slot_count = 2 * OBS_PATCH
    capacity = slot_count // tile_count
    cells = background.shape[3]

    states = lax.all_to_all(background, "mem", split_axis=1, concat_axis=0, tiled=True)
    flat_states = states.reshape(members, cells)
    state_sum = jnp.sum(flat_states.astype(jnp.float32), 0)
    state_mean = state_sum / members
    deviation = (flat_states.astype(jnp.float32) - state_mean[None, :]).astype(jnp.bfloat16)

    target = obs_patch[:, 0]
    slot_rank = rank_in_patch(target, patches)
    slot_place = target * capacity + slot_rank
    rows = jnp.concatenate(
        [evolved, jnp.stack([obs_value, obs_var, (obs_pos + 1).astype(jnp.bfloat16)])], 0
    )
    send = jnp.zeros((rows.shape[0], patches * capacity), jnp.bfloat16).at[:, slot_place].set(rows)
    got = lax.all_to_all(send, ("mem", "tile"), split_axis=1, concat_axis=1, tiled=True)
    got = got.reshape(rows.shape[0], mem_count, slot_count)
    gathered = got[:local_members].transpose(1, 0, 2).reshape(members, slot_count)
    got_info = got[local_members:, 0]

    obs_mean = jnp.sum(gathered.astype(jnp.float32), 0) / members
    centred = (gathered.astype(jnp.float32) - obs_mean[None, :]).astype(jnp.bfloat16)
    innovation = (got_info[0].astype(jnp.float32) - obs_mean).astype(jnp.bfloat16)
    stacked = jnp.concatenate([centred, innovation[None, :], got_info[1:3]], 0)
    axis = ("mem", "tile")
    next_mat, next_vec = block_terms(stacked, members, -1.0)
    prev_mat, prev_vec = block_terms(stacked, members, 1.0)
    from_prev = ring_shift(next_mat, axis, 1)
    from_prev_vec = ring_shift(next_vec, axis, 1)
    from_next = ring_shift(prev_mat, axis, -1)
    from_next_vec = ring_shift(prev_vec, axis, -1)
    own_mat, own_vec = block_terms(stacked, members, 0.0)
    gram_mat = own_mat + from_prev + from_next
    gram_vec = own_vec + from_prev_vec + from_next_vec
    transform_mat = transform(gram_mat, gram_vec)

    mixed = lax.dot_general(
        transform_mat, deviation, (((0,), (0,)), ((), ())), preferred_element_type=jnp.float32
    )
    updated = (state_mean[None, :] + mixed).astype(jnp.bfloat16)
    chunks = updated.reshape(mem_count, local_members, cells)
    me = lax.axis_index("mem")
    pieces = []
    for shift in range(mem_count):
        piece = lax.dynamic_index_in_dim(chunks, (me + shift) % mem_count, 0, keepdims=False)
        if shift:
            pairs = [(i, (i + shift) % mem_count) for i in range(mem_count)]
            piece = lax.ppermute(piece, "mem", pairs)
        pieces.append(piece)
    by_shift = jnp.stack(pieces)
    back = jnp.take(by_shift, (me - jnp.arange(mem_count)) % mem_count, axis=0)
    return back.transpose(1, 0, 2).reshape(local_members, mem_count, 1, cells)


def solution(mesh):
    return jax.shard_map(
        per_device,
        mesh=mesh,
        in_specs=(
            P("mem", None, "tile", None),
            P("mem", "tile"),
            P("tile"),
            P("tile"),
            P("tile", None),
            P("tile"),
        ),
        out_specs=P("mem", None, "tile", None),
        check_vma=False,
    )
```

```python
import functools
import math

import jax
import jax.numpy as jnp
from jax import lax
from jax.experimental import pallas as pl
from jax.sharding import PartitionSpec as P

PATCH_CELLS = 128
OBS_PATCH = 1024
ITERS = 4
HIGHEST = lax.Precision.HIGHEST
NEWTON = lax.Precision.HIGH


def ring_shift(block, axis, step):
    count = 1
    for name in axis:
        count *= lax.axis_size(name)
    pairs = [(i, (i + step) % count) for i in range(count)]
    return lax.ppermute(block, axis, pairs)


def localize(position, offset):
    distance = (offset * PATCH_CELLS + position + 0.5 - 0.5 * PATCH_CELLS) / PATCH_CELLS
    return jnp.exp(-2.0 * distance * distance)


def obs_weight(var_row, shifted_row):
    is_live = shifted_row.astype(jnp.float32) > 0.5
    safe_var = jnp.where(is_live, var_row.astype(jnp.float32), 1.0)
    return (jnp.where(is_live, 1.0 / safe_var, 0.0), shifted_row.astype(jnp.float32) - 1.0)


def block_terms(block, members, offset):
    centred = block[:members]
    innovation = block[members]
    weight, position = obs_weight(block[members + 1], block[members + 2])
    scale = weight * localize(position, offset)
    weighted = (centred.astype(jnp.float32) * scale[None, :]).astype(jnp.bfloat16)
    gram_mat = lax.dot_general(
        weighted, centred, (((1,), (1,)), ((), ())), preferred_element_type=jnp.float32
    )
    gram_vec = jnp.dot(weighted, innovation, preferred_element_type=jnp.float32)
    return gram_mat, gram_vec


def gram_kernel(x_ref, mat_ref, vec_ref, *, local_members, mem_count):
    step = pl.program_id(0)

    @pl.when(step == 0)
    def _():
        mat_ref[...] = jnp.zeros_like(mat_ref)
        vec_ref[...] = jnp.zeros_like(vec_ref)

    members = local_members * mem_count
    block = x_ref[...]
    values = block[:, 0, :local_members, :].reshape(members, block.shape[-1]).astype(jnp.float32)
    obs_mean = jnp.sum(values, 0, keepdims=True) / members
    centred = (values - obs_mean).astype(jnp.bfloat16)
    info = block[0, 0, local_members:local_members + 3, :].astype(jnp.float32)
    innovation = (info[0:1] - obs_mean).astype(jnp.bfloat16)
    is_live = info[2:3] > 0.5
    weight = jnp.where(is_live, 1.0 / jnp.where(is_live, info[1:2], 1.0), 0.0)
    position = info[2:3] - 1.0
    innov_rows = jnp.broadcast_to(innovation, (8, innovation.shape[1]))
    centred_f = centred.astype(jnp.float32)
    for index, offset in enumerate((-1.0, 0.0, 1.0)):
        scale = weight * localize(position, offset)
        weighted = (centred_f * scale).astype(jnp.bfloat16)
        mat_ref[index] += lax.dot_general(
            weighted, centred, (((1,), (1,)), ((), ())), preferred_element_type=jnp.float32
        )
        vec_ref[index] += lax.dot_general(
            innov_rows, weighted, (((1,), (1,)), ((), ())), preferred_element_type=jnp.float32
        )

def partial_grams(received, mem_count, tile_count, local_members):
    rows, slots = received.shape[1], received.shape[2]
    members = local_members * mem_count
    x = received.reshape(mem_count, tile_count, rows, slots)
    kernel = functools.partial(gram_kernel, local_members=local_members, mem_count=mem_count)
    mat, vec = pl.pallas_call(
        kernel,
        grid=(tile_count,),
        in_specs=[pl.BlockSpec((mem_count, 1, rows, slots), lambda t: (0, t, 0, 0))],
        out_specs=[
            pl.BlockSpec((3, members, members), lambda t: (0, 0, 0)),
            pl.BlockSpec((3, 8, members), lambda t: (0, 0, 0)),
        ],
        out_shape=[
            jax.ShapeDtypeStruct((3, members, members), jnp.float32),
            jax.ShapeDtypeStruct((3, 8, members), jnp.float32),
        ],
    )(x)
    return mat, vec[:, 0, :]


def inverse_root(gram_mat):
    mat_size = gram_mat.shape[0]
    identity = jnp.eye(mat_size, dtype=jnp.float32)
    norm_scale = jnp.sqrt(jnp.sum(gram_mat * gram_mat))
    root_up = gram_mat / norm_scale
    root_down = None
    for sweep_index in range(ITERS):
        if root_down is None:
            product = root_up
        else:
            product = jnp.dot(root_down, root_up, precision=NEWTON)
        middle = 1.5 * identity - 0.5 * product
        if sweep_index + 1 < ITERS:
            root_up = jnp.dot(root_up, middle, precision=NEWTON)
        root_down = middle if root_down is None else jnp.dot(middle, root_down, precision=NEWTON)
    return root_down / jnp.sqrt(norm_scale)


def transform(gram_mat, gram_vec):
    mat_size = gram_mat.shape[0]
    identity = jnp.eye(mat_size, dtype=jnp.float32)
    inv_root = inverse_root(gram_mat + (mat_size - 1.0) * identity)
    inner_w = jnp.dot(inv_root, gram_vec, precision=HIGHEST)
    mean_w = jnp.dot(inv_root, inner_w, precision=HIGHEST)
    return (math.sqrt(mat_size - 1.0) * inv_root + mean_w[:, None]).astype(jnp.bfloat16)


def rank_in_patch(target, patches):
    rows = target.shape[0]
    block = 128
    blocks = rows // block
    onehot = (target[:, None] == jnp.arange(patches, dtype=jnp.int32)[None, :]).astype(jnp.bfloat16)
    onehot = onehot.reshape(blocks, block, patches)
    lower = (jnp.arange(block)[:, None] >= jnp.arange(block)[None, :]).astype(jnp.bfloat16)
    within = jnp.einsum("ij,bjp->bip", lower, onehot, preferred_element_type=jnp.float32)
    totals = jnp.sum(onehot.astype(jnp.float32), 1)
    earlier = (jnp.arange(blocks)[:, None] > jnp.arange(blocks)[None, :]).astype(jnp.float32)
    before = jnp.dot(earlier, totals, precision=HIGHEST)
    count = jnp.sum((within + before[:, None, :]) * onehot.astype(jnp.float32), 2)
    return count.reshape(rows).astype(jnp.int32) - 1


def per_device(background, evolved, obs_value, obs_var, obs_patch, obs_pos):
    mem_count = lax.axis_size("mem")
    tile_count = lax.axis_size("tile")
    patches = mem_count * tile_count
    local_members = evolved.shape[0]
    members = local_members * mem_count
    slot_count = 2 * OBS_PATCH
    capacity = slot_count // tile_count
    cells = background.shape[3]

    states = lax.all_to_all(background, "mem", split_axis=1, concat_axis=0, tiled=True)
    flat_states = states.reshape(members, cells)
    state_sum = jnp.sum(flat_states.astype(jnp.float32), 0)
    state_mean = state_sum / members
    deviation = (flat_states.astype(jnp.float32) - state_mean[None, :]).astype(jnp.bfloat16)

    target = obs_patch[:, 0]
    slot_rank = rank_in_patch(target, patches)
    slot_place = target * capacity + slot_rank
    rows = jnp.concatenate(
        [evolved, jnp.stack([obs_value, obs_var, (obs_pos + 1).astype(jnp.bfloat16)])], 0
    )
    send = jnp.zeros((rows.shape[0], patches * capacity), jnp.bfloat16).at[:, slot_place].set(rows)
    send = send.reshape(rows.shape[0], patches, capacity).transpose(1, 0, 2)
    got = lax.all_to_all(send, ("mem", "tile"), split_axis=0, concat_axis=0, tiled=True)
    axis = ("mem", "tile")
    mats, vecs = partial_grams(got, mem_count, tile_count, local_members)
    next_mat, own_mat, prev_mat = mats[0], mats[1], mats[2]
    next_vec, own_vec, prev_vec = vecs[0], vecs[1], vecs[2]
    from_prev = ring_shift(next_mat, axis, 1)
    from_prev_vec = ring_shift(next_vec, axis, 1)
    from_next = ring_shift(prev_mat, axis, -1)
    from_next_vec = ring_shift(prev_vec, axis, -1)
    gram_mat = own_mat + from_prev + from_next
    gram_vec = own_vec + from_prev_vec + from_next_vec
    transform_mat = transform(gram_mat, gram_vec)

    mixed = lax.dot_general(
        transform_mat, deviation, (((0,), (0,)), ((), ())), preferred_element_type=jnp.float32
    )
    updated = (state_mean[None, :] + mixed).astype(jnp.bfloat16)
    chunks = updated.reshape(mem_count, local_members, cells)
    me = lax.axis_index("mem")
    pieces = []
    for shift in range(mem_count):
        piece = lax.dynamic_index_in_dim(chunks, (me + shift) % mem_count, 0, keepdims=False)
        if shift:
            pairs = [(i, (i + shift) % mem_count) for i in range(mem_count)]
            piece = lax.ppermute(piece, "mem", pairs)
        pieces.append(piece)
    by_shift = jnp.stack(pieces)
    back = jnp.take(by_shift, (me - jnp.arange(mem_count)) % mem_count, axis=0)
    return back.transpose(1, 0, 2).reshape(local_members, mem_count, 1, cells)


def solution(mesh):
    return jax.shard_map(
        per_device,
        mesh=mesh,
        in_specs=(
            P("mem", None, "tile", None),
            P("mem", "tile"),
            P("tile"),
            P("tile"),
            P("tile", None),
            P("tile"),
        ),
        out_specs=P("mem", None, "tile", None),
        check_vma=False,
    )
```

```python
import functools
import math

import jax
import jax.numpy as jnp
from jax import lax
from jax.experimental import pallas as pl
from jax.sharding import PartitionSpec as P

PATCH_CELLS = 128
OBS_PATCH = 1024
ITERS = 4
HIGHEST = lax.Precision.HIGHEST
NEWTON = lax.Precision.HIGH


def ring_shift(block, axis, step):
    count = 1
    for name in axis:
        count *= lax.axis_size(name)
    pairs = [(i, (i + step) % count) for i in range(count)]
    return lax.ppermute(block, axis, pairs)


def localize(position, offset):
    distance = (offset * PATCH_CELLS + position + 0.5 - 0.5 * PATCH_CELLS) / PATCH_CELLS
    return jnp.exp(-2.0 * distance * distance)


def obs_weight(var_row, shifted_row):
    is_live = shifted_row.astype(jnp.float32) > 0.5
    safe_var = jnp.where(is_live, var_row.astype(jnp.float32), 1.0)
    return (jnp.where(is_live, 1.0 / safe_var, 0.0), shifted_row.astype(jnp.float32) - 1.0)


def block_terms(block, members, offset):
    centred = block[:members]
    innovation = block[members]
    weight, position = obs_weight(block[members + 1], block[members + 2])
    scale = weight * localize(position, offset)
    weighted = (centred.astype(jnp.float32) * scale[None, :]).astype(jnp.bfloat16)
    gram_mat = lax.dot_general(
        weighted, centred, (((1,), (1,)), ((), ())), preferred_element_type=jnp.float32
    )
    gram_vec = jnp.dot(weighted, innovation, preferred_element_type=jnp.float32)
    return gram_mat, gram_vec


def gram_kernel(x_ref, mat_ref, vec_ref, *, local_members, mem_count, tiles_per_step):
    step = pl.program_id(0)

    @pl.when(step == 0)
    def _():
        mat_ref[...] = jnp.zeros_like(mat_ref)
        vec_ref[...] = jnp.zeros_like(vec_ref)

    members = local_members * mem_count
    block = x_ref[...]
    slots = block.shape[-1]
    values = jnp.concatenate(
        [block[:, j, :local_members, :].reshape(members, slots) for j in range(tiles_per_step)], 1
    ).astype(jnp.float32)
    info = jnp.concatenate(
        [block[0, j, local_members:local_members + 3, :] for j in range(tiles_per_step)], 1
    ).astype(jnp.float32)
    obs_mean = jnp.sum(values, 0, keepdims=True) / members
    centred = (values - obs_mean).astype(jnp.bfloat16)
    innovation = (info[0:1] - obs_mean).astype(jnp.bfloat16)
    is_live = info[2:3] > 0.5
    weight = jnp.where(is_live, 1.0 / jnp.where(is_live, info[1:2], 1.0), 0.0)
    position = info[2:3] - 1.0
    centred_f = centred.astype(jnp.float32)
    weighted = jnp.concatenate(
        [
            (centred_f * (weight * localize(position, offset))).astype(jnp.bfloat16)
            for offset in (-1.0, 0.0, 1.0)
        ],
        0,
    )
    mat_ref[...] += lax.dot_general(
        weighted, centred, (((1,), (1,)), ((), ())), preferred_element_type=jnp.float32
    )
    innov_rows = jnp.broadcast_to(innovation, (8, innovation.shape[1]))
    vec_ref[...] += lax.dot_general(
        innov_rows, weighted, (((1,), (1,)), ((), ())), preferred_element_type=jnp.float32
    )


def partial_grams(received, mem_count, tile_count, local_members):
    rows, slots = received.shape[1], received.shape[2]
    members = local_members * mem_count
    tiles_per_step = 2
    x = received.reshape(mem_count, tile_count, rows, slots)
    kernel = functools.partial(
        gram_kernel, local_members=local_members, mem_count=mem_count, tiles_per_step=tiles_per_step
    )
    mat, vec = pl.pallas_call(
        kernel,
        grid=(tile_count // tiles_per_step,),
        in_specs=[pl.BlockSpec((mem_count, tiles_per_step, rows, slots), lambda t: (0, t, 0, 0))],
        out_specs=[
            pl.BlockSpec((3 * members, members), lambda t: (0, 0)),
            pl.BlockSpec((8, 3 * members), lambda t: (0, 0)),
        ],
        out_shape=[
            jax.ShapeDtypeStruct((3 * members, members), jnp.float32),
            jax.ShapeDtypeStruct((8, 3 * members), jnp.float32),
        ],
    )(x)
    return mat.reshape(3, members, members), vec[0].reshape(3, members)


def inverse_root(gram_mat):
    mat_size = gram_mat.shape[0]
    identity = jnp.eye(mat_size, dtype=jnp.float32)
    norm_scale = jnp.sqrt(jnp.sum(gram_mat * gram_mat))
    root_up = gram_mat / norm_scale
    root_down = None
    for sweep_index in range(ITERS):
        if root_down is None:
            product = root_up
        else:
            product = jnp.dot(root_down, root_up, precision=NEWTON)
        middle = 1.5 * identity - 0.5 * product
        if sweep_index + 1 < ITERS:
            root_up = jnp.dot(root_up, middle, precision=NEWTON)
        root_down = middle if root_down is None else jnp.dot(middle, root_down, precision=NEWTON)
    return root_down / jnp.sqrt(norm_scale)


def transform(gram_mat, gram_vec):
    mat_size = gram_mat.shape[0]
    identity = jnp.eye(mat_size, dtype=jnp.float32)
    inv_root = inverse_root(gram_mat + (mat_size - 1.0) * identity)
    inner_w = jnp.dot(inv_root, gram_vec, precision=HIGHEST)
    mean_w = jnp.dot(inv_root, inner_w, precision=HIGHEST)
    return (math.sqrt(mat_size - 1.0) * inv_root + mean_w[:, None]).astype(jnp.bfloat16)


def rank_in_patch(target, patches):
    rows = target.shape[0]
    block = 128
    blocks = rows // block
    onehot = (target[:, None] == jnp.arange(patches, dtype=jnp.int32)[None, :]).astype(jnp.bfloat16)
    onehot = onehot.reshape(blocks, block, patches)
    lower = (jnp.arange(block)[:, None] >= jnp.arange(block)[None, :]).astype(jnp.bfloat16)
    within = jnp.einsum("ij,bjp->bip", lower, onehot, preferred_element_type=jnp.float32)
    totals = jnp.sum(onehot.astype(jnp.float32), 1)
    earlier = (jnp.arange(blocks)[:, None] > jnp.arange(blocks)[None, :]).astype(jnp.float32)
    before = jnp.dot(earlier, totals, precision=HIGHEST)
    count = jnp.sum((within + before[:, None, :]) * onehot.astype(jnp.float32), 2)
    return count.reshape(rows).astype(jnp.int32) - 1


def per_device(background, evolved, obs_value, obs_var, obs_patch, obs_pos):
    mem_count = lax.axis_size("mem")
    tile_count = lax.axis_size("tile")
    patches = mem_count * tile_count
    local_members = evolved.shape[0]
    members = local_members * mem_count
    slot_count = 2 * OBS_PATCH
    capacity = slot_count // tile_count
    cells = background.shape[3]

    states = lax.all_to_all(background, "mem", split_axis=1, concat_axis=0, tiled=True)
    flat_states = states.reshape(members, cells)
    state_sum = jnp.sum(flat_states.astype(jnp.float32), 0)
    state_mean = state_sum / members
    deviation = (flat_states.astype(jnp.float32) - state_mean[None, :]).astype(jnp.bfloat16)

    target = obs_patch[:, 0]
    slot_rank = rank_in_patch(target, patches)
    slot_place = target * capacity + slot_rank
    rows = jnp.concatenate(
        [evolved, jnp.stack([obs_value, obs_var, (obs_pos + 1).astype(jnp.bfloat16)])], 0
    )
    send = jnp.zeros((rows.shape[0], patches * capacity), jnp.bfloat16).at[:, slot_place].set(rows)
    send = send.reshape(rows.shape[0], patches, capacity).transpose(1, 0, 2)
    got = lax.all_to_all(send, ("mem", "tile"), split_axis=0, concat_axis=0, tiled=True)
    axis = ("mem", "tile")
    mats, vecs = partial_grams(got, mem_count, tile_count, local_members)
    next_mat, own_mat, prev_mat = mats[0], mats[1], mats[2]
    next_vec, own_vec, prev_vec = vecs[0], vecs[1], vecs[2]
    from_prev = ring_shift(next_mat, axis, 1)
    from_prev_vec = ring_shift(next_vec, axis, 1)
    from_next = ring_shift(prev_mat, axis, -1)
    from_next_vec = ring_shift(prev_vec, axis, -1)
    gram_mat = own_mat + from_prev + from_next
    gram_vec = own_vec + from_prev_vec + from_next_vec
    transform_mat = transform(gram_mat, gram_vec)

    mixed = lax.dot_general(
        transform_mat, deviation, (((0,), (0,)), ((), ())), preferred_element_type=jnp.float32
    )
    updated = (state_mean[None, :] + mixed).astype(jnp.bfloat16)
    chunks = updated.reshape(mem_count, local_members, cells)
    me = lax.axis_index("mem")
    pieces = []
    for shift in range(mem_count):
        piece = lax.dynamic_index_in_dim(chunks, (me + shift) % mem_count, 0, keepdims=False)
        if shift:
            pairs = [(i, (i + shift) % mem_count) for i in range(mem_count)]
            piece = lax.ppermute(piece, "mem", pairs)
        pieces.append(piece)
    by_shift = jnp.stack(pieces)
    back = jnp.take(by_shift, (me - jnp.arange(mem_count)) % mem_count, axis=0)
    return back.transpose(1, 0, 2).reshape(local_members, mem_count, 1, cells)


def solution(mesh):
    return jax.shard_map(
        per_device,
        mesh=mesh,
        in_specs=(
            P("mem", None, "tile", None),
            P("mem", "tile"),
            P("tile"),
            P("tile"),
            P("tile", None),
            P("tile"),
        ),
        out_specs=P("mem", None, "tile", None),
        check_vma=False,
    )
```

```python
import functools
import math

import jax
import jax.numpy as jnp
from jax import lax
from jax.experimental import pallas as pl
from jax.sharding import PartitionSpec as P

PATCH_CELLS = 128
OBS_PATCH = 1024
ITERS = 4
HIGHEST = lax.Precision.HIGHEST
NEWTON = lax.Precision.HIGH


def ring_shift(block, axis, step):
    count = 1
    for name in axis:
        count *= lax.axis_size(name)
    pairs = [(i, (i + step) % count) for i in range(count)]
    return lax.ppermute(block, axis, pairs)


def localize(position, offset):
    distance = (offset * PATCH_CELLS + position + 0.5 - 0.5 * PATCH_CELLS) / PATCH_CELLS
    return jnp.exp(-2.0 * distance * distance)


def obs_weight(var_row, shifted_row):
    is_live = shifted_row.astype(jnp.float32) > 0.5
    safe_var = jnp.where(is_live, var_row.astype(jnp.float32), 1.0)
    return (jnp.where(is_live, 1.0 / safe_var, 0.0), shifted_row.astype(jnp.float32) - 1.0)


def block_terms(block, members, offset):
    centred = block[:members]
    innovation = block[members]
    weight, position = obs_weight(block[members + 1], block[members + 2])
    scale = weight * localize(position, offset)
    weighted = (centred.astype(jnp.float32) * scale[None, :]).astype(jnp.bfloat16)
    gram_mat = lax.dot_general(
        weighted, centred, (((1,), (1,)), ((), ())), preferred_element_type=jnp.float32
    )
    gram_vec = jnp.dot(weighted, innovation, preferred_element_type=jnp.float32)
    return gram_mat, gram_vec


def gram_kernel(x_ref, mat_ref, vec_ref, *, local_members, mem_count, tiles_per_step):
    step = pl.program_id(0)

    @pl.when(step == 0)
    def _():
        mat_ref[...] = jnp.zeros_like(mat_ref)
        vec_ref[...] = jnp.zeros_like(vec_ref)

    members = local_members * mem_count
    block = x_ref[...]
    slots = block.shape[-1]
    values = jnp.concatenate(
        [block[:, j, :local_members, :].reshape(members, slots) for j in range(tiles_per_step)], 1
    ).astype(jnp.float32)
    info = jnp.concatenate(
        [block[0, j, local_members:local_members + 3, :] for j in range(tiles_per_step)], 1
    ).astype(jnp.float32)
    obs_mean = jnp.sum(values, 0, keepdims=True) / members
    centred = (values - obs_mean).astype(jnp.bfloat16)
    innovation = (info[0:1] - obs_mean).astype(jnp.bfloat16)
    is_live = info[2:3] > 0.5
    weight = jnp.where(is_live, 1.0 / jnp.where(is_live, info[1:2], 1.0), 0.0)
    position = info[2:3] - 1.0
    centred_f = centred.astype(jnp.float32)
    weighted = jnp.concatenate(
        [
            (centred_f * (weight * localize(position, offset))).astype(jnp.bfloat16)
            for offset in (-1.0, 0.0, 1.0)
        ],
        0,
    )
    mat_ref[...] += lax.dot_general(
        weighted, centred, (((1,), (1,)), ((), ())), preferred_element_type=jnp.float32
    )
    innov_rows = jnp.broadcast_to(innovation, (8, innovation.shape[1]))
    vec_ref[...] += lax.dot_general(
        innov_rows, weighted, (((1,), (1,)), ((), ())), preferred_element_type=jnp.float32
    )


def partial_grams(received, mem_count, tile_count, local_members):
    rows, slots = received.shape[1], received.shape[2]
    members = local_members * mem_count
    tiles_per_step = 2
    x = received.reshape(mem_count, tile_count, rows, slots)
    kernel = functools.partial(
        gram_kernel, local_members=local_members, mem_count=mem_count, tiles_per_step=tiles_per_step
    )
    mat, vec = pl.pallas_call(
        kernel,
        grid=(tile_count // tiles_per_step,),
        in_specs=[pl.BlockSpec((mem_count, tiles_per_step, rows, slots), lambda t: (0, t, 0, 0))],
        out_specs=[
            pl.BlockSpec((3 * members, members), lambda t: (0, 0)),
            pl.BlockSpec((8, 3 * members), lambda t: (0, 0)),
        ],
        out_shape=[
            jax.ShapeDtypeStruct((3 * members, members), jnp.float32),
            jax.ShapeDtypeStruct((8, 3 * members), jnp.float32),
        ],
    )(x)
    return mat.reshape(3, members, members), vec[0].reshape(3, members)


def inverse_root(gram_mat):
    mat_size = gram_mat.shape[0]
    identity = jnp.eye(mat_size, dtype=jnp.float32)
    norm_scale = jnp.sqrt(jnp.sum(gram_mat * gram_mat))
    root_up = gram_mat / norm_scale
    root_down = None
    for sweep_index in range(ITERS):
        if root_down is None:
            product = root_up
        else:
            product = jnp.dot(root_down, root_up, precision=NEWTON)
        middle = 1.5 * identity - 0.5 * product
        if sweep_index + 1 < ITERS:
            root_up = jnp.dot(root_up, middle, precision=NEWTON)
        root_down = middle if root_down is None else jnp.dot(middle, root_down, precision=NEWTON)
    return root_down / jnp.sqrt(norm_scale)


def transform(gram_mat, gram_vec):
    mat_size = gram_mat.shape[0]
    identity = jnp.eye(mat_size, dtype=jnp.float32)
    inv_root = inverse_root(gram_mat + (mat_size - 1.0) * identity)
    inner_w = jnp.dot(inv_root, gram_vec, precision=HIGHEST)
    mean_w = jnp.dot(inv_root, inner_w, precision=HIGHEST)
    return (math.sqrt(mat_size - 1.0) * inv_root + mean_w[:, None]).astype(jnp.bfloat16)


def rank_in_patch(target, patches):
    rows = target.shape[0]
    block = 128
    blocks = rows // block
    onehot = (target[:, None] == jnp.arange(patches, dtype=jnp.int32)[None, :]).astype(jnp.bfloat16)
    onehot = onehot.reshape(blocks, block, patches)
    lower = (jnp.arange(block)[:, None] >= jnp.arange(block)[None, :]).astype(jnp.bfloat16)
    within = jnp.einsum("ij,bjp->bip", lower, onehot, preferred_element_type=jnp.float32)
    totals = jnp.sum(onehot.astype(jnp.float32), 1)
    earlier = (jnp.arange(blocks)[:, None] > jnp.arange(blocks)[None, :]).astype(jnp.float32)
    before = jnp.dot(earlier, totals, precision=HIGHEST)
    count = jnp.sum((within + before[:, None, :]) * onehot.astype(jnp.float32), 2)
    return count.reshape(rows).astype(jnp.int32) - 1


def per_device(background, evolved, obs_value, obs_var, obs_patch, obs_pos):
    mem_count = lax.axis_size("mem")
    tile_count = lax.axis_size("tile")
    patches = mem_count * tile_count
    local_members = evolved.shape[0]
    members = local_members * mem_count
    slot_count = 2 * OBS_PATCH
    capacity = slot_count // tile_count
    cells = background.shape[3]

    target = obs_patch[:, 0]
    slot_rank = rank_in_patch(target, patches)
    slot_place = target * capacity + slot_rank
    rows = jnp.concatenate(
        [evolved, jnp.stack([obs_value, obs_var, (obs_pos + 1).astype(jnp.bfloat16)])], 0
    )
    send = jnp.zeros((rows.shape[0], patches * capacity), jnp.bfloat16).at[:, slot_place].set(rows)
    send = send.reshape(rows.shape[0], patches, capacity).transpose(1, 0, 2)
    got = lax.all_to_all(send, ("mem", "tile"), split_axis=0, concat_axis=0, tiled=True)
    axis = ("mem", "tile")
    mats, vecs = partial_grams(got, mem_count, tile_count, local_members)
    background, mats = lax.optimization_barrier((background, mats))
    next_mat, own_mat, prev_mat = mats[0], mats[1], mats[2]
    states = lax.all_to_all(background, "mem", split_axis=1, concat_axis=0, tiled=True)
    flat_states = states.reshape(members, cells)
    state_sum = jnp.sum(flat_states.astype(jnp.float32), 0)
    state_mean = state_sum / members
    deviation = (flat_states.astype(jnp.float32) - state_mean[None, :]).astype(jnp.bfloat16)

    next_vec, own_vec, prev_vec = vecs[0], vecs[1], vecs[2]
    from_prev = ring_shift(next_mat, axis, 1)
    from_prev_vec = ring_shift(next_vec, axis, 1)
    from_next = ring_shift(prev_mat, axis, -1)
    from_next_vec = ring_shift(prev_vec, axis, -1)
    gram_mat = own_mat + from_prev + from_next
    gram_vec = own_vec + from_prev_vec + from_next_vec
    transform_mat = transform(gram_mat, gram_vec)

    mixed = lax.dot_general(
        transform_mat, deviation, (((0,), (0,)), ((), ())), preferred_element_type=jnp.float32
    )
    updated = (state_mean[None, :] + mixed).astype(jnp.bfloat16)
    chunks = updated.reshape(mem_count, local_members, cells)
    me = lax.axis_index("mem")
    pieces = []
    for shift in range(mem_count):
        piece = lax.dynamic_index_in_dim(chunks, (me + shift) % mem_count, 0, keepdims=False)
        if shift:
            pairs = [(i, (i + shift) % mem_count) for i in range(mem_count)]
            piece = lax.ppermute(piece, "mem", pairs)
        pieces.append(piece)
    by_shift = jnp.stack(pieces)
    back = jnp.take(by_shift, (me - jnp.arange(mem_count)) % mem_count, axis=0)
    return back.transpose(1, 0, 2).reshape(local_members, mem_count, 1, cells)


def solution(mesh):
    return jax.shard_map(
        per_device,
        mesh=mesh,
        in_specs=(
            P("mem", None, "tile", None),
            P("mem", "tile"),
            P("tile"),
            P("tile"),
            P("tile", None),
            P("tile"),
        ),
        out_specs=P("mem", None, "tile", None),
        check_vma=False,
    )
```

```python
import functools
import math

import jax
import jax.numpy as jnp
from jax import lax
from jax.experimental import pallas as pl
from jax.sharding import PartitionSpec as P

PATCH_CELLS = 128
OBS_PATCH = 1024
ITERS = 4
HIGHEST = lax.Precision.HIGHEST
NEWTON = lax.Precision.HIGH


def ring_shift(block, axis, step):
    count = 1
    for name in axis:
        count *= lax.axis_size(name)
    pairs = [(i, (i + step) % count) for i in range(count)]
    return lax.ppermute(block, axis, pairs)


def localize(position, offset):
    distance = (offset * PATCH_CELLS + position + 0.5 - 0.5 * PATCH_CELLS) / PATCH_CELLS
    return jnp.exp(-2.0 * distance * distance)


def obs_weight(var_row, shifted_row):
    is_live = shifted_row.astype(jnp.float32) > 0.5
    safe_var = jnp.where(is_live, var_row.astype(jnp.float32), 1.0)
    return (jnp.where(is_live, 1.0 / safe_var, 0.0), shifted_row.astype(jnp.float32) - 1.0)


def block_terms(block, members, offset):
    centred = block[:members]
    innovation = block[members]
    weight, position = obs_weight(block[members + 1], block[members + 2])
    scale = weight * localize(position, offset)
    weighted = (centred.astype(jnp.float32) * scale[None, :]).astype(jnp.bfloat16)
    gram_mat = lax.dot_general(
        weighted, centred, (((1,), (1,)), ((), ())), preferred_element_type=jnp.float32
    )
    gram_vec = jnp.dot(weighted, innovation, preferred_element_type=jnp.float32)
    return gram_mat, gram_vec


def gram_kernel(x_ref, mat_ref, vec_ref, *, local_members, mem_count, tiles_per_step):
    step = pl.program_id(0)

    @pl.when(step == 0)
    def _():
        mat_ref[...] = jnp.zeros_like(mat_ref)
        vec_ref[...] = jnp.zeros_like(vec_ref)

    members = local_members * mem_count
    block = x_ref[...]
    slots = block.shape[-1]
    values = jnp.concatenate(
        [block[:, j, :local_members, :].reshape(members, slots) for j in range(tiles_per_step)], 1
    ).astype(jnp.float32)
    info = jnp.concatenate(
        [block[0, j, local_members:local_members + 3, :] for j in range(tiles_per_step)], 1
    ).astype(jnp.float32)
    obs_mean = jnp.sum(values, 0, keepdims=True) / members
    centred = (values - obs_mean).astype(jnp.bfloat16)
    innovation = (info[0:1] - obs_mean).astype(jnp.bfloat16)
    is_live = info[2:3] > 0.5
    weight = jnp.where(is_live, 1.0 / jnp.where(is_live, info[1:2], 1.0), 0.0)
    position = info[2:3] - 1.0
    centred_f = centred.astype(jnp.float32)
    weighted = jnp.concatenate(
        [
            (centred_f * (weight * localize(position, offset))).astype(jnp.bfloat16)
            for offset in (-1.0, 0.0, 1.0)
        ],
        0,
    )
    mat_ref[...] += lax.dot_general(
        weighted, centred, (((1,), (1,)), ((), ())), preferred_element_type=jnp.float32
    )
    innov_rows = jnp.broadcast_to(innovation, (8, innovation.shape[1]))
    vec_ref[...] += lax.dot_general(
        innov_rows, weighted, (((1,), (1,)), ((), ())), preferred_element_type=jnp.float32
    )


def partial_grams(received, mem_count, tile_count, local_members):
    rows, slots = received.shape[1], received.shape[2]
    members = local_members * mem_count
    tiles_per_step = 2
    x = received.reshape(mem_count, tile_count, rows, slots)
    kernel = functools.partial(
        gram_kernel, local_members=local_members, mem_count=mem_count, tiles_per_step=tiles_per_step
    )
    mat, vec = pl.pallas_call(
        kernel,
        grid=(tile_count // tiles_per_step,),
        in_specs=[pl.BlockSpec((mem_count, tiles_per_step, rows, slots), lambda t: (0, t, 0, 0))],
        out_specs=[
            pl.BlockSpec((3 * members, members), lambda t: (0, 0)),
            pl.BlockSpec((8, 3 * members), lambda t: (0, 0)),
        ],
        out_shape=[
            jax.ShapeDtypeStruct((3 * members, members), jnp.float32),
            jax.ShapeDtypeStruct((8, 3 * members), jnp.float32),
        ],
    )(x)
    return mat.reshape(3, members, members), vec[0].reshape(3, members)


def inverse_root(gram_mat):
    mat_size = gram_mat.shape[0]
    identity = jnp.eye(mat_size, dtype=jnp.float32)
    norm_scale = jnp.sqrt(jnp.sum(gram_mat * gram_mat))
    root_up = gram_mat / norm_scale
    root_down = None
    for sweep_index in range(ITERS):
        if root_down is None:
            product = root_up
        else:
            product = jnp.dot(root_down, root_up, precision=NEWTON)
        middle = 1.5 * identity - 0.5 * product
        if sweep_index + 1 < ITERS:
            root_up = jnp.dot(root_up, middle, precision=NEWTON)
        root_down = middle if root_down is None else jnp.dot(middle, root_down, precision=NEWTON)
    return root_down / jnp.sqrt(norm_scale)


def transform(gram_mat, gram_vec):
    mat_size = gram_mat.shape[0]
    identity = jnp.eye(mat_size, dtype=jnp.float32)
    inv_root = inverse_root(gram_mat + (mat_size - 1.0) * identity)
    inner_w = jnp.dot(inv_root, gram_vec, precision=HIGHEST)
    mean_w = jnp.dot(inv_root, inner_w, precision=HIGHEST)
    return (math.sqrt(mat_size - 1.0) * inv_root + mean_w[:, None]).astype(jnp.bfloat16)


def rank_in_patch(target, patches):
    rows = target.shape[0]
    block = 128
    blocks = rows // block
    onehot = (target[:, None] == jnp.arange(patches, dtype=jnp.int32)[None, :]).astype(jnp.bfloat16)
    onehot = onehot.reshape(blocks, block, patches)
    lower = (jnp.arange(block)[:, None] >= jnp.arange(block)[None, :]).astype(jnp.bfloat16)
    within = jnp.einsum("ij,bjp->bip", lower, onehot, preferred_element_type=jnp.float32)
    totals = jnp.sum(onehot.astype(jnp.float32), 1)
    earlier = (jnp.arange(blocks)[:, None] > jnp.arange(blocks)[None, :]).astype(jnp.float32)
    before = jnp.dot(earlier, totals, precision=HIGHEST)
    count = jnp.sum((within + before[:, None, :]) * onehot.astype(jnp.float32), 2)
    return count.reshape(rows).astype(jnp.int32) - 1


def per_device(background, evolved, obs_value, obs_var, obs_patch, obs_pos):
    mem_count = lax.axis_size("mem")
    tile_count = lax.axis_size("tile")
    patches = mem_count * tile_count
    local_members = evolved.shape[0]
    members = local_members * mem_count
    slot_count = 2 * OBS_PATCH
    capacity = slot_count // tile_count
    cells = background.shape[3]

    target = obs_patch[:, 0]
    slot_rank = rank_in_patch(target, patches)
    slot_place = target * capacity + slot_rank
    rows = jnp.concatenate(
        [evolved, jnp.stack([obs_value, obs_var, (obs_pos + 1).astype(jnp.bfloat16)])], 0
    )
    send = jnp.zeros((rows.shape[0], patches * capacity), jnp.bfloat16).at[:, slot_place].set(rows)
    send = send.reshape(rows.shape[0], patches, capacity).transpose(1, 0, 2)
    got = lax.all_to_all(send, ("mem", "tile"), split_axis=0, concat_axis=0, tiled=True)
    axis = ("mem", "tile")
    mats, vecs = partial_grams(got, mem_count, tile_count, local_members)
    next_mat, own_mat, prev_mat = mats[0], mats[1], mats[2]
    next_vec, own_vec, prev_vec = vecs[0], vecs[1], vecs[2]
    from_prev = ring_shift(next_mat, axis, 1)
    from_prev_vec = ring_shift(next_vec, axis, 1)
    from_next = ring_shift(prev_mat, axis, -1)
    from_next_vec = ring_shift(prev_vec, axis, -1)
    gram_mat = own_mat + from_prev + from_next
    gram_vec = own_vec + from_prev_vec + from_next_vec
    background, gram_mat, gram_vec = lax.optimization_barrier((background, gram_mat, gram_vec))
    states = lax.all_to_all(background, "mem", split_axis=1, concat_axis=0, tiled=True)
    flat_states = states.reshape(members, cells)
    state_sum = jnp.sum(flat_states.astype(jnp.float32), 0)
    state_mean = state_sum / members
    deviation = (flat_states.astype(jnp.float32) - state_mean[None, :]).astype(jnp.bfloat16)

    transform_mat = transform(gram_mat, gram_vec)

    mixed = lax.dot_general(
        transform_mat, deviation, (((0,), (0,)), ((), ())), preferred_element_type=jnp.float32
    )
    updated = (state_mean[None, :] + mixed).astype(jnp.bfloat16)
    chunks = updated.reshape(mem_count, local_members, cells)
    me = lax.axis_index("mem")
    pieces = []
    for shift in range(mem_count):
        piece = lax.dynamic_index_in_dim(chunks, (me + shift) % mem_count, 0, keepdims=False)
        if shift:
            pairs = [(i, (i + shift) % mem_count) for i in range(mem_count)]
            piece = lax.ppermute(piece, "mem", pairs)
        pieces.append(piece)
    by_shift = jnp.stack(pieces)
    back = jnp.take(by_shift, (me - jnp.arange(mem_count)) % mem_count, axis=0)
    return back.transpose(1, 0, 2).reshape(local_members, mem_count, 1, cells)


def solution(mesh):
    return jax.shard_map(
        per_device,
        mesh=mesh,
        in_specs=(
            P("mem", None, "tile", None),
            P("mem", "tile"),
            P("tile"),
            P("tile"),
            P("tile", None),
            P("tile"),
        ),
        out_specs=P("mem", None, "tile", None),
        check_vma=False,
    )
```

```python
import functools
import math

import jax
import jax.numpy as jnp
from jax import lax
from jax.experimental import pallas as pl
from jax.sharding import PartitionSpec as P

PATCH_CELLS = 128
OBS_PATCH = 1024
ITERS = 4
HIGHEST = lax.Precision.HIGHEST
NEWTON = lax.Precision.HIGH


def ring_shift(block, axis, step):
    count = 1
    for name in axis:
        count *= lax.axis_size(name)
    pairs = [(i, (i + step) % count) for i in range(count)]
    return lax.ppermute(block, axis, pairs)


def localize(position, offset):
    distance = (offset * PATCH_CELLS + position + 0.5 - 0.5 * PATCH_CELLS) / PATCH_CELLS
    return jnp.exp(-2.0 * distance * distance)


def obs_weight(var_row, shifted_row):
    is_live = shifted_row.astype(jnp.float32) > 0.5
    safe_var = jnp.where(is_live, var_row.astype(jnp.float32), 1.0)
    return (jnp.where(is_live, 1.0 / safe_var, 0.0), shifted_row.astype(jnp.float32) - 1.0)


def block_terms(block, members, offset):
    centred = block[:members]
    innovation = block[members]
    weight, position = obs_weight(block[members + 1], block[members + 2])
    scale = weight * localize(position, offset)
    weighted = (centred.astype(jnp.float32) * scale[None, :]).astype(jnp.bfloat16)
    gram_mat = lax.dot_general(
        weighted, centred, (((1,), (1,)), ((), ())), preferred_element_type=jnp.float32
    )
    gram_vec = jnp.dot(weighted, innovation, preferred_element_type=jnp.float32)
    return gram_mat, gram_vec


def gram_kernel(x_ref, mat_ref, vec_ref, *, local_members, mem_count, tiles_per_step, offsets):
    step = pl.program_id(0)

    @pl.when(step == 0)
    def _():
        mat_ref[...] = jnp.zeros_like(mat_ref)
        vec_ref[...] = jnp.zeros_like(vec_ref)

    members = local_members * mem_count
    block = x_ref[...]
    slots = block.shape[-1]
    values = jnp.concatenate(
        [block[:, j, :local_members, :].reshape(members, slots) for j in range(tiles_per_step)], 1
    ).astype(jnp.float32)
    info = jnp.concatenate(
        [block[0, j, local_members:local_members + 3, :] for j in range(tiles_per_step)], 1
    ).astype(jnp.float32)
    obs_mean = jnp.sum(values, 0, keepdims=True) / members
    centred = (values - obs_mean).astype(jnp.bfloat16)
    innovation = (info[0:1] - obs_mean).astype(jnp.bfloat16)
    is_live = info[2:3] > 0.5
    weight = jnp.where(is_live, 1.0 / jnp.where(is_live, info[1:2], 1.0), 0.0)
    position = info[2:3] - 1.0
    centred_f = centred.astype(jnp.float32)
    weighted = jnp.concatenate(
        [
            (centred_f * (weight * localize(position, offset))).astype(jnp.bfloat16)
            for offset in offsets
        ],
        0,
    )
    mat_ref[...] += lax.dot_general(
        weighted, centred, (((1,), (1,)), ((), ())), preferred_element_type=jnp.float32
    )
    innov_rows = jnp.broadcast_to(innovation, (8, innovation.shape[1]))
    vec_ref[...] += lax.dot_general(
        innov_rows, weighted, (((1,), (1,)), ((), ())), preferred_element_type=jnp.float32
    )


def partial_grams(received, mem_count, tile_count, local_members, offsets):
    rows, slots = received.shape[1], received.shape[2]
    members = local_members * mem_count
    tiles_per_step = 2
    x = received.reshape(mem_count, tile_count, rows, slots)
    kernel = functools.partial(
        gram_kernel,
        local_members=local_members,
        mem_count=mem_count,
        tiles_per_step=tiles_per_step,
        offsets=offsets,
    )
    count = len(offsets)
    mat, vec = pl.pallas_call(
        kernel,
        grid=(tile_count // tiles_per_step,),
        in_specs=[pl.BlockSpec((mem_count, tiles_per_step, rows, slots), lambda t: (0, t, 0, 0))],
        out_specs=[
            pl.BlockSpec((count * members, members), lambda t: (0, 0)),
            pl.BlockSpec((8, count * members), lambda t: (0, 0)),
        ],
        out_shape=[
            jax.ShapeDtypeStruct((count * members, members), jnp.float32),
            jax.ShapeDtypeStruct((8, count * members), jnp.float32),
        ],
    )(x)
    return mat.reshape(count, members, members), vec[0].reshape(count, members)


def inverse_root(gram_mat):
    mat_size = gram_mat.shape[0]
    identity = jnp.eye(mat_size, dtype=jnp.float32)
    norm_scale = jnp.sqrt(jnp.sum(gram_mat * gram_mat))
    root_up = gram_mat / norm_scale
    root_down = None
    for sweep_index in range(ITERS):
        if root_down is None:
            product = root_up
        else:
            product = jnp.dot(root_down, root_up, precision=NEWTON)
        middle = 1.5 * identity - 0.5 * product
        if sweep_index + 1 < ITERS:
            root_up = jnp.dot(root_up, middle, precision=NEWTON)
        root_down = middle if root_down is None else jnp.dot(middle, root_down, precision=NEWTON)
    return root_down / jnp.sqrt(norm_scale)


def transform(gram_mat, gram_vec):
    mat_size = gram_mat.shape[0]
    identity = jnp.eye(mat_size, dtype=jnp.float32)
    inv_root = inverse_root(gram_mat + (mat_size - 1.0) * identity)
    inner_w = jnp.dot(inv_root, gram_vec, precision=HIGHEST)
    mean_w = jnp.dot(inv_root, inner_w, precision=HIGHEST)
    return (math.sqrt(mat_size - 1.0) * inv_root + mean_w[:, None]).astype(jnp.bfloat16)


def rank_in_patch(target, patches):
    rows = target.shape[0]
    block = 128
    blocks = rows // block
    onehot = (target[:, None] == jnp.arange(patches, dtype=jnp.int32)[None, :]).astype(jnp.bfloat16)
    onehot = onehot.reshape(blocks, block, patches)
    lower = (jnp.arange(block)[:, None] >= jnp.arange(block)[None, :]).astype(jnp.bfloat16)
    within = jnp.einsum("ij,bjp->bip", lower, onehot, preferred_element_type=jnp.float32)
    totals = jnp.sum(onehot.astype(jnp.float32), 1)
    earlier = (jnp.arange(blocks)[:, None] > jnp.arange(blocks)[None, :]).astype(jnp.float32)
    before = jnp.dot(earlier, totals, precision=HIGHEST)
    count = jnp.sum((within + before[:, None, :]) * onehot.astype(jnp.float32), 2)
    return count.reshape(rows).astype(jnp.int32) - 1


def per_device(background, evolved, obs_value, obs_var, obs_patch, obs_pos):
    mem_count = lax.axis_size("mem")
    tile_count = lax.axis_size("tile")
    patches = mem_count * tile_count
    local_members = evolved.shape[0]
    members = local_members * mem_count
    slot_count = 2 * OBS_PATCH
    capacity = slot_count // tile_count
    cells = background.shape[3]

    states = lax.all_to_all(background, "mem", split_axis=1, concat_axis=0, tiled=True)
    flat_states = states.reshape(members, cells)
    state_sum = jnp.sum(flat_states.astype(jnp.float32), 0)
    state_mean = state_sum / members
    deviation = (flat_states.astype(jnp.float32) - state_mean[None, :]).astype(jnp.bfloat16)

    target = obs_patch[:, 0]
    slot_rank = rank_in_patch(target, patches)
    slot_place = target * capacity + slot_rank
    rows = jnp.concatenate(
        [evolved, jnp.stack([obs_value, obs_var, (obs_pos + 1).astype(jnp.bfloat16)])], 0
    )
    send = jnp.zeros((rows.shape[0], patches * capacity), jnp.bfloat16).at[:, slot_place].set(rows)
    send = send.reshape(rows.shape[0], patches, capacity).transpose(1, 0, 2)
    got = lax.all_to_all(send, ("mem", "tile"), split_axis=0, concat_axis=0, tiled=True)
    axis = ("mem", "tile")
    mats, vecs = partial_grams(got, mem_count, tile_count, local_members, (-1.0, 1.0))
    next_mat, prev_mat = mats[0], mats[1]
    next_vec, prev_vec = vecs[0], vecs[1]
    from_prev = ring_shift(next_mat, axis, 1)
    from_prev_vec = ring_shift(next_vec, axis, 1)
    from_next = ring_shift(prev_mat, axis, -1)
    from_next_vec = ring_shift(prev_vec, axis, -1)
    own_mats, own_vecs = partial_grams(got, mem_count, tile_count, local_members, (0.0,))
    own_mat, own_vec = own_mats[0], own_vecs[0]
    gram_mat = own_mat + from_prev + from_next
    gram_vec = own_vec + from_prev_vec + from_next_vec
    transform_mat = transform(gram_mat, gram_vec)

    mixed = lax.dot_general(
        transform_mat, deviation, (((0,), (0,)), ((), ())), preferred_element_type=jnp.float32
    )
    updated = (state_mean[None, :] + mixed).astype(jnp.bfloat16)
    chunks = updated.reshape(mem_count, local_members, cells)
    me = lax.axis_index("mem")
    pieces = []
    for shift in range(mem_count):
        piece = lax.dynamic_index_in_dim(chunks, (me + shift) % mem_count, 0, keepdims=False)
        if shift:
            pairs = [(i, (i + shift) % mem_count) for i in range(mem_count)]
            piece = lax.ppermute(piece, "mem", pairs)
        pieces.append(piece)
    by_shift = jnp.stack(pieces)
    back = jnp.take(by_shift, (me - jnp.arange(mem_count)) % mem_count, axis=0)
    return back.transpose(1, 0, 2).reshape(local_members, mem_count, 1, cells)


def solution(mesh):
    return jax.shard_map(
        per_device,
        mesh=mesh,
        in_specs=(
            P("mem", None, "tile", None),
            P("mem", "tile"),
            P("tile"),
            P("tile"),
            P("tile", None),
            P("tile"),
        ),
        out_specs=P("mem", None, "tile", None),
        check_vma=False,
    )
```

```python
import functools
import math

import jax
import jax.numpy as jnp
from jax import lax
from jax.experimental import pallas as pl
from jax.sharding import PartitionSpec as P

PATCH_CELLS = 128
OBS_PATCH = 1024
ITERS = 4
HIGHEST = lax.Precision.HIGHEST
NEWTON = lax.Precision.HIGH


def ring_shift(block, axis, step):
    count = 1
    for name in axis:
        count *= lax.axis_size(name)
    pairs = [(i, (i + step) % count) for i in range(count)]
    return lax.ppermute(block, axis, pairs)


def localize(position, offset):
    distance = (offset * PATCH_CELLS + position + 0.5 - 0.5 * PATCH_CELLS) / PATCH_CELLS
    return jnp.exp(-2.0 * distance * distance)


def obs_weight(var_row, shifted_row):
    is_live = shifted_row.astype(jnp.float32) > 0.5
    safe_var = jnp.where(is_live, var_row.astype(jnp.float32), 1.0)
    return (jnp.where(is_live, 1.0 / safe_var, 0.0), shifted_row.astype(jnp.float32) - 1.0)


def block_terms(block, members, offset):
    centred = block[:members]
    innovation = block[members]
    weight, position = obs_weight(block[members + 1], block[members + 2])
    scale = weight * localize(position, offset)
    weighted = (centred.astype(jnp.float32) * scale[None, :]).astype(jnp.bfloat16)
    gram_mat = lax.dot_general(
        weighted, centred, (((1,), (1,)), ((), ())), preferred_element_type=jnp.float32
    )
    gram_vec = jnp.dot(weighted, innovation, preferred_element_type=jnp.float32)
    return gram_mat, gram_vec


def gram_kernel(x_ref, mat_ref, vec_ref, *, local_members, mem_count, tiles_per_step):
    step = pl.program_id(0)

    @pl.when(step == 0)
    def _():
        mat_ref[...] = jnp.zeros_like(mat_ref)
        vec_ref[...] = jnp.zeros_like(vec_ref)

    members = local_members * mem_count
    block = x_ref[...]
    slots = block.shape[-1]
    values = jnp.concatenate(
        [block[:, j, :local_members, :].reshape(members, slots) for j in range(tiles_per_step)], 1
    ).astype(jnp.float32)
    info = jnp.concatenate(
        [block[0, j, local_members:local_members + 3, :] for j in range(tiles_per_step)], 1
    ).astype(jnp.float32)
    obs_mean = jnp.sum(values, 0, keepdims=True) / members
    centred = (values - obs_mean).astype(jnp.bfloat16)
    innovation = (info[0:1] - obs_mean).astype(jnp.bfloat16)
    is_live = info[2:3] > 0.5
    weight = jnp.where(is_live, 1.0 / jnp.where(is_live, info[1:2], 1.0), 0.0)
    position = info[2:3] - 1.0
    centred_f = centred.astype(jnp.float32)
    weighted = jnp.concatenate(
        [
            (centred_f * (weight * localize(position, offset))).astype(jnp.bfloat16)
            for offset in (-1.0, 0.0, 1.0)
        ],
        0,
    )
    mat_ref[...] += lax.dot_general(
        weighted, centred, (((1,), (1,)), ((), ())), preferred_element_type=jnp.float32
    )
    innov_rows = jnp.broadcast_to(innovation, (8, innovation.shape[1]))
    vec_ref[...] += lax.dot_general(
        innov_rows, weighted, (((1,), (1,)), ((), ())), preferred_element_type=jnp.float32
    )


def partial_grams(received, mem_count, tile_count, local_members):
    rows, slots = received.shape[1], received.shape[2]
    members = local_members * mem_count
    tiles_per_step = 2
    x = received.reshape(mem_count, tile_count, rows, slots)
    kernel = functools.partial(
        gram_kernel, local_members=local_members, mem_count=mem_count, tiles_per_step=tiles_per_step
    )
    mat, vec = pl.pallas_call(
        kernel,
        grid=(tile_count // tiles_per_step,),
        in_specs=[pl.BlockSpec((mem_count, tiles_per_step, rows, slots), lambda t: (0, t, 0, 0))],
        out_specs=[
            pl.BlockSpec((3 * members, members), lambda t: (0, 0)),
            pl.BlockSpec((8, 3 * members), lambda t: (0, 0)),
        ],
        out_shape=[
            jax.ShapeDtypeStruct((3 * members, members), jnp.float32),
            jax.ShapeDtypeStruct((8, 3 * members), jnp.float32),
        ],
    )(x)
    return mat.reshape(3, members, members), vec[0].reshape(3, members)


def inverse_root(gram_mat):
    mat_size = gram_mat.shape[0]
    identity = jnp.eye(mat_size, dtype=jnp.float32)
    norm_scale = jnp.sqrt(jnp.sum(gram_mat * gram_mat))
    root_up = gram_mat / norm_scale
    root_down = None
    for sweep_index in range(ITERS):
        if root_down is None:
            product = root_up
        else:
            product = jnp.dot(root_down, root_up, precision=NEWTON)
        middle = 1.5 * identity - 0.5 * product
        if sweep_index + 1 < ITERS:
            root_up = jnp.dot(root_up, middle, precision=NEWTON)
        root_down = middle if root_down is None else jnp.dot(middle, root_down, precision=NEWTON)
    return root_down / jnp.sqrt(norm_scale)


def transform(gram_mat, gram_vec):
    mat_size = gram_mat.shape[0]
    identity = jnp.eye(mat_size, dtype=jnp.float32)
    inv_root = inverse_root(gram_mat + (mat_size - 1.0) * identity)
    inner_w = jnp.dot(inv_root, gram_vec, precision=HIGHEST)
    mean_w = jnp.dot(inv_root, inner_w, precision=HIGHEST)
    return (math.sqrt(mat_size - 1.0) * inv_root + mean_w[:, None]).astype(jnp.bfloat16)


def rank_in_patch(target, patches):
    rows = target.shape[0]
    block = 128
    blocks = rows // block
    onehot = (target[:, None] == jnp.arange(patches, dtype=jnp.int32)[None, :]).astype(jnp.bfloat16)
    onehot = onehot.reshape(blocks, block, patches)
    lower = (jnp.arange(block)[:, None] >= jnp.arange(block)[None, :]).astype(jnp.bfloat16)
    within = jnp.einsum("ij,bjp->bip", lower, onehot, preferred_element_type=jnp.float32)
    totals = jnp.sum(onehot.astype(jnp.float32), 1)
    earlier = (jnp.arange(blocks)[:, None] > jnp.arange(blocks)[None, :]).astype(jnp.float32)
    before = jnp.dot(earlier, totals, precision=HIGHEST)
    count = jnp.sum((within + before[:, None, :]) * onehot.astype(jnp.float32), 2)
    return count.reshape(rows).astype(jnp.int32) - 1


def per_device(background, evolved, obs_value, obs_var, obs_patch, obs_pos):
    mem_count = lax.axis_size("mem")
    tile_count = lax.axis_size("tile")
    patches = mem_count * tile_count
    local_members = evolved.shape[0]
    members = local_members * mem_count
    slot_count = 2 * OBS_PATCH
    capacity = slot_count // tile_count
    cells = background.shape[3]

    states = lax.all_to_all(background, "mem", split_axis=1, concat_axis=0, tiled=True)
    flat_states = states.reshape(members, cells)
    state_sum = jnp.sum(flat_states.astype(jnp.float32), 0)
    state_mean = state_sum / members
    deviation = (flat_states.astype(jnp.float32) - state_mean[None, :]).astype(jnp.bfloat16)

    target = obs_patch[:, 0]
    slot_rank = rank_in_patch(target, patches)
    slot_place = target * capacity + slot_rank
    rows = jnp.concatenate(
        [evolved, jnp.stack([obs_value, obs_var, (obs_pos + 1).astype(jnp.bfloat16)])], 0
    )
    send = jnp.zeros((rows.shape[0], patches * capacity), jnp.bfloat16).at[:, slot_place].set(rows)
    send = send.reshape(rows.shape[0], patches, capacity).transpose(1, 0, 2)
    got = lax.all_to_all(send, ("mem", "tile"), split_axis=0, concat_axis=0, tiled=True)
    axis = ("mem", "tile")
    mats, vecs = partial_grams(got, mem_count, tile_count, local_members)
    next_mat, own_mat, prev_mat = mats[0], mats[1], mats[2]
    next_vec, own_vec, prev_vec = vecs[0], vecs[1], vecs[2]
    diag_mask = jnp.eye(members, dtype=jnp.bool_)
    from_prev = ring_shift(next_mat.astype(jnp.bfloat16), axis, 1)
    from_prev_side = ring_shift(jnp.stack([next_vec, jnp.diagonal(next_mat)]), axis, 1)
    from_next = ring_shift(prev_mat.astype(jnp.bfloat16), axis, -1)
    from_next_side = ring_shift(jnp.stack([prev_vec, jnp.diagonal(prev_mat)]), axis, -1)
    from_prev = jnp.where(diag_mask, from_prev_side[1][None, :], from_prev.astype(jnp.float32))
    from_next = jnp.where(diag_mask, from_next_side[1][None, :], from_next.astype(jnp.float32))
    gram_mat = own_mat + from_prev + from_next
    gram_vec = own_vec + from_prev_side[0] + from_next_side[0]
    transform_mat = transform(gram_mat, gram_vec)

    mixed = lax.dot_general(
        transform_mat, deviation, (((0,), (0,)), ((), ())), preferred_element_type=jnp.float32
    )
    updated = (state_mean[None, :] + mixed).astype(jnp.bfloat16)
    chunks = updated.reshape(mem_count, local_members, cells)
    me = lax.axis_index("mem")
    pieces = []
    for shift in range(mem_count):
        piece = lax.dynamic_index_in_dim(chunks, (me + shift) % mem_count, 0, keepdims=False)
        if shift:
            pairs = [(i, (i + shift) % mem_count) for i in range(mem_count)]
            piece = lax.ppermute(piece, "mem", pairs)
        pieces.append(piece)
    by_shift = jnp.stack(pieces)
    back = jnp.take(by_shift, (me - jnp.arange(mem_count)) % mem_count, axis=0)
    return back.transpose(1, 0, 2).reshape(local_members, mem_count, 1, cells)


def solution(mesh):
    return jax.shard_map(
        per_device,
        mesh=mesh,
        in_specs=(
            P("mem", None, "tile", None),
            P("mem", "tile"),
            P("tile"),
            P("tile"),
            P("tile", None),
            P("tile"),
        ),
        out_specs=P("mem", None, "tile", None),
        check_vma=False,
    )
```

```python
import functools
import math

import jax
import jax.numpy as jnp
from jax import lax
from jax.experimental import pallas as pl
from jax.sharding import PartitionSpec as P

PATCH_CELLS = 128
OBS_PATCH = 1024
ITERS = 4
HIGHEST = lax.Precision.HIGHEST
NEWTON = lax.Precision.HIGH


def ring_shift(block, axis, step):
    count = 1
    for name in axis:
        count *= lax.axis_size(name)
    pairs = [(i, (i + step) % count) for i in range(count)]
    return lax.ppermute(block, axis, pairs)


def localize(position, offset):
    distance = (offset * PATCH_CELLS + position + 0.5 - 0.5 * PATCH_CELLS) / PATCH_CELLS
    return jnp.exp(-2.0 * distance * distance)


def obs_weight(var_row, shifted_row):
    is_live = shifted_row.astype(jnp.float32) > 0.5
    safe_var = jnp.where(is_live, var_row.astype(jnp.float32), 1.0)
    return (jnp.where(is_live, 1.0 / safe_var, 0.0), shifted_row.astype(jnp.float32) - 1.0)


def block_terms(block, members, offset):
    centred = block[:members]
    innovation = block[members]
    weight, position = obs_weight(block[members + 1], block[members + 2])
    scale = weight * localize(position, offset)
    weighted = (centred.astype(jnp.float32) * scale[None, :]).astype(jnp.bfloat16)
    gram_mat = lax.dot_general(
        weighted, centred, (((1,), (1,)), ((), ())), preferred_element_type=jnp.float32
    )
    gram_vec = jnp.dot(weighted, innovation, preferred_element_type=jnp.float32)
    return gram_mat, gram_vec


def gram_kernel(x_ref, mat_ref, vec_ref, *, local_members, mem_count, tiles_per_step):
    step = pl.program_id(0)

    @pl.when(step == 0)
    def _():
        mat_ref[...] = jnp.zeros_like(mat_ref)
        vec_ref[...] = jnp.zeros_like(vec_ref)

    members = local_members * mem_count
    block = x_ref[...]
    slots = block.shape[-1]
    values = jnp.concatenate(
        [block[:, j, :local_members, :].reshape(members, slots) for j in range(tiles_per_step)], 1
    ).astype(jnp.float32)
    info = jnp.concatenate(
        [block[0, j, local_members:local_members + 3, :] for j in range(tiles_per_step)], 1
    ).astype(jnp.float32)
    obs_mean = jnp.sum(values, 0, keepdims=True) / members
    centred = (values - obs_mean).astype(jnp.bfloat16)
    innovation = (info[0:1] - obs_mean).astype(jnp.bfloat16)
    is_live = info[2:3] > 0.5
    weight = jnp.where(is_live, 1.0 / jnp.where(is_live, info[1:2], 1.0), 0.0)
    position = info[2:3] - 1.0
    centred_f = centred.astype(jnp.float32)
    weighted = jnp.concatenate(
        [
            (centred_f * (weight * localize(position, offset))).astype(jnp.bfloat16)
            for offset in (-1.0, 0.0, 1.0)
        ],
        0,
    )
    mat_ref[...] += lax.dot_general(
        weighted, centred, (((1,), (1,)), ((), ())), preferred_element_type=jnp.float32
    )
    innov_rows = jnp.broadcast_to(innovation, (8, innovation.shape[1]))
    vec_ref[...] += lax.dot_general(
        innov_rows, weighted, (((1,), (1,)), ((), ())), preferred_element_type=jnp.float32
    )


def partial_grams(received, mem_count, tile_count, local_members):
    rows, slots = received.shape[1], received.shape[2]
    members = local_members * mem_count
    tiles_per_step = 2
    x = received.reshape(mem_count, tile_count, rows, slots)
    kernel = functools.partial(
        gram_kernel, local_members=local_members, mem_count=mem_count, tiles_per_step=tiles_per_step
    )
    mat, vec = pl.pallas_call(
        kernel,
        grid=(tile_count // tiles_per_step,),
        in_specs=[pl.BlockSpec((mem_count, tiles_per_step, rows, slots), lambda t: (0, t, 0, 0))],
        out_specs=[
            pl.BlockSpec((3 * members, members), lambda t: (0, 0)),
            pl.BlockSpec((8, 3 * members), lambda t: (0, 0)),
        ],
        out_shape=[
            jax.ShapeDtypeStruct((3 * members, members), jnp.float32),
            jax.ShapeDtypeStruct((8, 3 * members), jnp.float32),
        ],
    )(x)
    return mat.reshape(3, members, members), vec[0].reshape(3, members)


def inverse_root(gram_mat):
    mat_size = gram_mat.shape[0]
    identity = jnp.eye(mat_size, dtype=jnp.float32)
    norm_scale = jnp.sqrt(jnp.sum(gram_mat * gram_mat))
    root_up = gram_mat / norm_scale
    root_down = None
    for sweep_index in range(ITERS):
        if root_down is None:
            product = root_up
        else:
            product = jnp.dot(root_down, root_up, precision=NEWTON)
        middle = 1.5 * identity - 0.5 * product
        if sweep_index + 1 < ITERS:
            root_up = jnp.dot(root_up, middle, precision=NEWTON)
        root_down = middle if root_down is None else jnp.dot(middle, root_down, precision=NEWTON)
    return root_down / jnp.sqrt(norm_scale)


def transform(gram_mat, gram_vec):
    mat_size = gram_mat.shape[0]
    identity = jnp.eye(mat_size, dtype=jnp.float32)
    inv_root = inverse_root(gram_mat + (mat_size - 1.0) * identity)
    inner_w = jnp.dot(inv_root, gram_vec, precision=HIGHEST)
    mean_w = jnp.dot(inv_root, inner_w, precision=HIGHEST)
    return (math.sqrt(mat_size - 1.0) * inv_root + mean_w[:, None]).astype(jnp.bfloat16)


def rank_in_patch(target, patches):
    rows = target.shape[0]
    block = 128
    blocks = rows // block
    onehot = (target[:, None] == jnp.arange(patches, dtype=jnp.int32)[None, :]).astype(jnp.bfloat16)
    onehot = onehot.reshape(blocks, block, patches)
    lower = (jnp.arange(block)[:, None] >= jnp.arange(block)[None, :]).astype(jnp.bfloat16)
    within = jnp.einsum("ij,bjp->bip", lower, onehot, preferred_element_type=jnp.float32)
    totals = jnp.sum(onehot.astype(jnp.float32), 1)
    earlier = (jnp.arange(blocks)[:, None] > jnp.arange(blocks)[None, :]).astype(jnp.float32)
    before = jnp.dot(earlier, totals, precision=HIGHEST)
    count = jnp.sum((within + before[:, None, :]) * onehot.astype(jnp.float32), 2)
    return count.reshape(rows).astype(jnp.int32) - 1


def per_device(background, evolved, obs_value, obs_var, obs_patch, obs_pos):
    mem_count = lax.axis_size("mem")
    tile_count = lax.axis_size("tile")
    patches = mem_count * tile_count
    local_members = evolved.shape[0]
    members = local_members * mem_count
    slot_count = 2 * OBS_PATCH
    capacity = slot_count // tile_count
    cells = background.shape[3]

    states = lax.all_to_all(background, "mem", split_axis=1, concat_axis=0, tiled=True)
    flat_states = states.reshape(members, cells)
    state_sum = jnp.sum(flat_states.astype(jnp.float32), 0)
    state_mean = state_sum / members
    deviation = (flat_states.astype(jnp.float32) - state_mean[None, :]).astype(jnp.bfloat16)

    target = obs_patch[:, 0]
    slot_rank = rank_in_patch(target, patches)
    slot_place = target * capacity + slot_rank
    rows = jnp.concatenate(
        [evolved, jnp.stack([obs_value, obs_var, (obs_pos + 1).astype(jnp.bfloat16)])], 0
    )
    send = jnp.zeros((rows.shape[0], patches * capacity), jnp.bfloat16).at[:, slot_place].set(rows)
    send = send.reshape(rows.shape[0], patches, capacity).transpose(1, 0, 2)
    got = lax.all_to_all(send, ("mem", "tile"), split_axis=0, concat_axis=0, tiled=True)
    axis = ("mem", "tile")
    mats, vecs = partial_grams(got, mem_count, tile_count, local_members)
    next_mat, own_mat, prev_mat = mats[0], mats[1], mats[2]
    next_vec, own_vec, prev_vec = vecs[0], vecs[1], vecs[2]
    diag_mask = jnp.eye(members, dtype=jnp.bool_)
    from_prev = ring_shift(next_mat.astype(jnp.bfloat16), axis, 1)
    from_prev_side = ring_shift(jnp.stack([next_vec, jnp.sum(jnp.where(diag_mask, next_mat, 0.0), 0)]), axis, 1)
    from_next = ring_shift(prev_mat.astype(jnp.bfloat16), axis, -1)
    from_next_side = ring_shift(jnp.stack([prev_vec, jnp.sum(jnp.where(diag_mask, prev_mat, 0.0), 0)]), axis, -1)
    from_prev = jnp.where(diag_mask, from_prev_side[1][None, :], from_prev.astype(jnp.float32))
    from_next = jnp.where(diag_mask, from_next_side[1][None, :], from_next.astype(jnp.float32))
    gram_mat = own_mat + from_prev + from_next
    gram_vec = own_vec + from_prev_side[0] + from_next_side[0]
    transform_mat = transform(gram_mat, gram_vec)

    mixed = lax.dot_general(
        transform_mat, deviation, (((0,), (0,)), ((), ())), preferred_element_type=jnp.float32
    )
    updated = (state_mean[None, :] + mixed).astype(jnp.bfloat16)
    chunks = updated.reshape(mem_count, local_members, cells)
    me = lax.axis_index("mem")
    pieces = []
    for shift in range(mem_count):
        piece = lax.dynamic_index_in_dim(chunks, (me + shift) % mem_count, 0, keepdims=False)
        if shift:
            pairs = [(i, (i + shift) % mem_count) for i in range(mem_count)]
            piece = lax.ppermute(piece, "mem", pairs)
        pieces.append(piece)
    by_shift = jnp.stack(pieces)
    back = jnp.take(by_shift, (me - jnp.arange(mem_count)) % mem_count, axis=0)
    return back.transpose(1, 0, 2).reshape(local_members, mem_count, 1, cells)


def solution(mesh):
    return jax.shard_map(
        per_device,
        mesh=mesh,
        in_specs=(
            P("mem", None, "tile", None),
            P("mem", "tile"),
            P("tile"),
            P("tile"),
            P("tile", None),
            P("tile"),
        ),
        out_specs=P("mem", None, "tile", None),
        check_vma=False,
    )
```

```python
import functools
import math

import jax
import jax.numpy as jnp
from jax import lax
from jax.experimental import pallas as pl
from jax.sharding import PartitionSpec as P

PATCH_CELLS = 128
OBS_PATCH = 1024
ITERS = 4
HIGHEST = lax.Precision.HIGHEST
NEWTON = lax.Precision.HIGH


def ring_shift(block, axis, step):
    count = 1
    for name in axis:
        count *= lax.axis_size(name)
    pairs = [(i, (i + step) % count) for i in range(count)]
    return lax.ppermute(block, axis, pairs)


def localize(position, offset):
    distance = (offset * PATCH_CELLS + position + 0.5 - 0.5 * PATCH_CELLS) / PATCH_CELLS
    return jnp.exp(-2.0 * distance * distance)


def obs_weight(var_row, shifted_row):
    is_live = shifted_row.astype(jnp.float32) > 0.5
    safe_var = jnp.where(is_live, var_row.astype(jnp.float32), 1.0)
    return (jnp.where(is_live, 1.0 / safe_var, 0.0), shifted_row.astype(jnp.float32) - 1.0)


def block_terms(block, members, offset):
    centred = block[:members]
    innovation = block[members]
    weight, position = obs_weight(block[members + 1], block[members + 2])
    scale = weight * localize(position, offset)
    weighted = (centred.astype(jnp.float32) * scale[None, :]).astype(jnp.bfloat16)
    gram_mat = lax.dot_general(
        weighted, centred, (((1,), (1,)), ((), ())), preferred_element_type=jnp.float32
    )
    gram_vec = jnp.dot(weighted, innovation, preferred_element_type=jnp.float32)
    return gram_mat, gram_vec


def gram_kernel(x_ref, mat_ref, vec_ref, *, local_members, mem_count, tiles_per_step):
    step = pl.program_id(0)

    @pl.when(step == 0)
    def _():
        mat_ref[...] = jnp.zeros_like(mat_ref)
        vec_ref[...] = jnp.zeros_like(vec_ref)

    members = local_members * mem_count
    block = x_ref[...]
    slots = block.shape[-1]
    values = jnp.concatenate(
        [block[:, j, :local_members, :].reshape(members, slots) for j in range(tiles_per_step)], 1
    ).astype(jnp.float32)
    info = jnp.concatenate(
        [block[0, j, local_members:local_members + 3, :] for j in range(tiles_per_step)], 1
    ).astype(jnp.float32)
    obs_mean = jnp.sum(values, 0, keepdims=True) / members
    centred = (values - obs_mean).astype(jnp.bfloat16)
    innovation = (info[0:1] - obs_mean).astype(jnp.bfloat16)
    is_live = info[2:3] > 0.5
    weight = jnp.where(is_live, 1.0 / jnp.where(is_live, info[1:2], 1.0), 0.0)
    position = info[2:3] - 1.0
    centred_f = centred.astype(jnp.float32)
    weighted = jnp.concatenate(
        [
            (centred_f * (weight * localize(position, offset))).astype(jnp.bfloat16)
            for offset in (-1.0, 0.0, 1.0)
        ],
        0,
    )
    mat_ref[...] += lax.dot_general(
        weighted, centred, (((1,), (1,)), ((), ())), preferred_element_type=jnp.float32
    )
    innov_rows = jnp.broadcast_to(innovation, (8, innovation.shape[1]))
    vec_ref[...] += lax.dot_general(
        innov_rows, weighted, (((1,), (1,)), ((), ())), preferred_element_type=jnp.float32
    )


def partial_grams(received, mem_count, tile_count, local_members):
    rows, slots = received.shape[1], received.shape[2]
    members = local_members * mem_count
    tiles_per_step = 2
    x = received.reshape(mem_count, tile_count, rows, slots)
    kernel = functools.partial(
        gram_kernel, local_members=local_members, mem_count=mem_count, tiles_per_step=tiles_per_step
    )
    mat, vec = pl.pallas_call(
        kernel,
        grid=(tile_count // tiles_per_step,),
        in_specs=[pl.BlockSpec((mem_count, tiles_per_step, rows, slots), lambda t: (0, t, 0, 0))],
        out_specs=[
            pl.BlockSpec((3 * members, members), lambda t: (0, 0)),
            pl.BlockSpec((8, 3 * members), lambda t: (0, 0)),
        ],
        out_shape=[
            jax.ShapeDtypeStruct((3 * members, members), jnp.float32),
            jax.ShapeDtypeStruct((8, 3 * members), jnp.float32),
        ],
    )(x)
    return mat.reshape(3, members, members), vec[0].reshape(3, members)


def inverse_root(gram_mat):
    mat_size = gram_mat.shape[0]
    identity = jnp.eye(mat_size, dtype=jnp.float32)
    norm_scale = jnp.sqrt(jnp.sum(gram_mat * gram_mat))
    root_up = gram_mat / norm_scale
    root_down = None
    for sweep_index in range(ITERS):
        if root_down is None:
            product = root_up
        else:
            product = jnp.dot(root_down, root_up, precision=NEWTON)
        middle = 1.5 * identity - 0.5 * product
        if sweep_index + 1 < ITERS:
            root_up = jnp.dot(root_up, middle, precision=NEWTON)
        root_down = middle if root_down is None else jnp.dot(middle, root_down, precision=NEWTON)
    return root_down / jnp.sqrt(norm_scale)


def transform(gram_mat, gram_vec):
    mat_size = gram_mat.shape[0]
    identity = jnp.eye(mat_size, dtype=jnp.float32)
    inv_root = inverse_root(gram_mat + (mat_size - 1.0) * identity)
    inner_w = jnp.dot(inv_root, gram_vec, precision=HIGHEST)
    mean_w = jnp.dot(inv_root, inner_w, precision=HIGHEST)
    return (math.sqrt(mat_size - 1.0) * inv_root + mean_w[:, None]).astype(jnp.bfloat16)


def rank_in_patch(target, patches):
    rows = target.shape[0]
    block = 128
    blocks = rows // block
    onehot = (target[:, None] == jnp.arange(patches, dtype=jnp.int32)[None, :]).astype(jnp.bfloat16)
    onehot = onehot.reshape(blocks, block, patches)
    lower = (jnp.arange(block)[:, None] >= jnp.arange(block)[None, :]).astype(jnp.bfloat16)
    within = jnp.einsum("ij,bjp->bip", lower, onehot, preferred_element_type=jnp.float32)
    totals = jnp.sum(onehot.astype(jnp.float32), 1)
    earlier = (jnp.arange(blocks)[:, None] > jnp.arange(blocks)[None, :]).astype(jnp.float32)
    before = jnp.dot(earlier, totals, precision=HIGHEST)
    count = jnp.sum((within + before[:, None, :]) * onehot.astype(jnp.float32), 2)
    return count.reshape(rows).astype(jnp.int32) - 1


def exchange_mem(chunks, dim):
    count = lax.axis_size("mem")
    me = lax.axis_index("mem")
    pieces = []
    for shift in range(count):
        piece = lax.dynamic_index_in_dim(chunks, (me + shift) % count, dim, keepdims=False)
        if shift:
            pairs = [(i, (i + shift) % count) for i in range(count)]
            piece = lax.ppermute(piece, "mem", pairs)
        pieces.append(piece)
    by_shift = jnp.stack(pieces)
    return jnp.take(by_shift, (me - jnp.arange(count)) % count, axis=0)


def per_device(background, evolved, obs_value, obs_var, obs_patch, obs_pos):
    mem_count = lax.axis_size("mem")
    tile_count = lax.axis_size("tile")
    patches = mem_count * tile_count
    local_members = evolved.shape[0]
    members = local_members * mem_count
    slot_count = 2 * OBS_PATCH
    capacity = slot_count // tile_count
    cells = background.shape[3]

    flat_states = exchange_mem(background.reshape(local_members, mem_count, cells), 1).reshape(members, cells)
    state_sum = jnp.sum(flat_states.astype(jnp.float32), 0)
    state_mean = state_sum / members
    deviation = (flat_states.astype(jnp.float32) - state_mean[None, :]).astype(jnp.bfloat16)

    target = obs_patch[:, 0]
    slot_rank = rank_in_patch(target, patches)
    slot_place = target * capacity + slot_rank
    rows = jnp.concatenate(
        [evolved, jnp.stack([obs_value, obs_var, (obs_pos + 1).astype(jnp.bfloat16)])], 0
    )
    send = jnp.zeros((rows.shape[0], patches * capacity), jnp.bfloat16).at[:, slot_place].set(rows)
    send = send.reshape(rows.shape[0], patches, capacity).transpose(1, 0, 2)
    got = lax.all_to_all(send, ("mem", "tile"), split_axis=0, concat_axis=0, tiled=True)
    axis = ("mem", "tile")
    mats, vecs = partial_grams(got, mem_count, tile_count, local_members)
    next_mat, own_mat, prev_mat = mats[0], mats[1], mats[2]
    next_vec, own_vec, prev_vec = vecs[0], vecs[1], vecs[2]
    diag_mask = jnp.eye(members, dtype=jnp.bool_)
    from_prev = ring_shift(next_mat.astype(jnp.bfloat16), axis, 1)
    from_prev_side = ring_shift(jnp.stack([next_vec, jnp.sum(jnp.where(diag_mask, next_mat, 0.0), 0)]), axis, 1)
    from_next = ring_shift(prev_mat.astype(jnp.bfloat16), axis, -1)
    from_next_side = ring_shift(jnp.stack([prev_vec, jnp.sum(jnp.where(diag_mask, prev_mat, 0.0), 0)]), axis, -1)
    from_prev = jnp.where(diag_mask, from_prev_side[1][None, :], from_prev.astype(jnp.float32))
    from_next = jnp.where(diag_mask, from_next_side[1][None, :], from_next.astype(jnp.float32))
    gram_mat = own_mat + from_prev + from_next
    gram_vec = own_vec + from_prev_side[0] + from_next_side[0]
    transform_mat = transform(gram_mat, gram_vec)

    mixed = lax.dot_general(
        transform_mat, deviation, (((0,), (0,)), ((), ())), preferred_element_type=jnp.float32
    )
    updated = (state_mean[None, :] + mixed).astype(jnp.bfloat16)
    back = exchange_mem(updated.reshape(mem_count, local_members, cells), 0)
    return back.transpose(1, 0, 2).reshape(local_members, mem_count, 1, cells)


def solution(mesh):
    return jax.shard_map(
        per_device,
        mesh=mesh,
        in_specs=(
            P("mem", None, "tile", None),
            P("mem", "tile"),
            P("tile"),
            P("tile"),
            P("tile", None),
            P("tile"),
        ),
        out_specs=P("mem", None, "tile", None),
        check_vma=False,
    )
```

```python
import functools
import math

import jax
import jax.numpy as jnp
from jax import lax
from jax.experimental import pallas as pl
from jax.sharding import PartitionSpec as P

PATCH_CELLS = 128
OBS_PATCH = 1024
ITERS = 4
HIGHEST = lax.Precision.HIGHEST
NEWTON = lax.Precision.HIGH


def ring_shift(block, axis, step):
    count = 1
    for name in axis:
        count *= lax.axis_size(name)
    pairs = [(i, (i + step) % count) for i in range(count)]
    return lax.ppermute(block, axis, pairs)


def localize(position, offset):
    distance = (offset * PATCH_CELLS + position + 0.5 - 0.5 * PATCH_CELLS) / PATCH_CELLS
    return jnp.exp(-2.0 * distance * distance)


def obs_weight(var_row, shifted_row):
    is_live = shifted_row.astype(jnp.float32) > 0.5
    safe_var = jnp.where(is_live, var_row.astype(jnp.float32), 1.0)
    return (jnp.where(is_live, 1.0 / safe_var, 0.0), shifted_row.astype(jnp.float32) - 1.0)


def block_terms(block, members, offset):
    centred = block[:members]
    innovation = block[members]
    weight, position = obs_weight(block[members + 1], block[members + 2])
    scale = weight * localize(position, offset)
    weighted = (centred.astype(jnp.float32) * scale[None, :]).astype(jnp.bfloat16)
    gram_mat = lax.dot_general(
        weighted, centred, (((1,), (1,)), ((), ())), preferred_element_type=jnp.float32
    )
    gram_vec = jnp.dot(weighted, innovation, preferred_element_type=jnp.float32)
    return gram_mat, gram_vec


def gram_kernel(x_ref, mat_ref, vec_ref, *, local_members, mem_count, tiles_per_step):
    step = pl.program_id(0)

    @pl.when(step == 0)
    def _():
        mat_ref[...] = jnp.zeros_like(mat_ref)
        vec_ref[...] = jnp.zeros_like(vec_ref)

    members = local_members * mem_count
    block = x_ref[...]
    slots = block.shape[-1]
    values = jnp.concatenate(
        [block[:, j, :local_members, :].reshape(members, slots) for j in range(tiles_per_step)], 1
    ).astype(jnp.float32)
    info = jnp.concatenate(
        [block[0, j, local_members:local_members + 3, :] for j in range(tiles_per_step)], 1
    ).astype(jnp.float32)
    obs_mean = jnp.sum(values, 0, keepdims=True) / members
    centred = (values - obs_mean).astype(jnp.bfloat16)
    innovation = (info[0:1] - obs_mean).astype(jnp.bfloat16)
    is_live = info[2:3] > 0.5
    weight = jnp.where(is_live, 1.0 / jnp.where(is_live, info[1:2], 1.0), 0.0)
    position = info[2:3] - 1.0
    centred_f = centred.astype(jnp.float32)
    weighted = jnp.concatenate(
        [
            (centred_f * (weight * localize(position, offset))).astype(jnp.bfloat16)
            for offset in (-1.0, 0.0, 1.0)
        ],
        0,
    )
    mat_ref[...] += lax.dot_general(
        weighted, centred, (((1,), (1,)), ((), ())), preferred_element_type=jnp.float32
    )
    innov_rows = jnp.broadcast_to(innovation, (8, innovation.shape[1]))
    vec_ref[...] += lax.dot_general(
        innov_rows, weighted, (((1,), (1,)), ((), ())), preferred_element_type=jnp.float32
    )


def partial_grams(received, mem_count, tile_count, local_members):
    rows, slots = received.shape[1], received.shape[2]
    members = local_members * mem_count
    tiles_per_step = 2
    x = received.reshape(mem_count, tile_count, rows, slots)
    kernel = functools.partial(
        gram_kernel, local_members=local_members, mem_count=mem_count, tiles_per_step=tiles_per_step
    )
    mat, vec = pl.pallas_call(
        kernel,
        grid=(tile_count // tiles_per_step,),
        in_specs=[pl.BlockSpec((mem_count, tiles_per_step, rows, slots), lambda t: (0, t, 0, 0))],
        out_specs=[
            pl.BlockSpec((3 * members, members), lambda t: (0, 0)),
            pl.BlockSpec((8, 3 * members), lambda t: (0, 0)),
        ],
        out_shape=[
            jax.ShapeDtypeStruct((3 * members, members), jnp.float32),
            jax.ShapeDtypeStruct((8, 3 * members), jnp.float32),
        ],
    )(x)
    return mat.reshape(3, members, members), vec[0].reshape(3, members)


def inverse_root(gram_mat):
    mat_size = gram_mat.shape[0]
    identity = jnp.eye(mat_size, dtype=jnp.float32)
    norm_scale = jnp.sqrt(jnp.sum(gram_mat * gram_mat))
    root_up = gram_mat / norm_scale
    root_down = None
    for sweep_index in range(ITERS):
        if root_down is None:
            product = root_up
        else:
            product = jnp.dot(root_down, root_up, precision=NEWTON)
        middle = 1.5 * identity - 0.5 * product
        if sweep_index + 1 < ITERS:
            root_up = jnp.dot(root_up, middle, precision=NEWTON)
        root_down = middle if root_down is None else jnp.dot(middle, root_down, precision=NEWTON)
    return root_down / jnp.sqrt(norm_scale)


def transform(gram_mat, gram_vec):
    mat_size = gram_mat.shape[0]
    identity = jnp.eye(mat_size, dtype=jnp.float32)
    inv_root = inverse_root(gram_mat + (mat_size - 1.0) * identity)
    inner_w = jnp.dot(inv_root, gram_vec, precision=HIGHEST)
    mean_w = jnp.dot(inv_root, inner_w, precision=HIGHEST)
    return (math.sqrt(mat_size - 1.0) * inv_root + mean_w[:, None]).astype(jnp.bfloat16)


def rank_in_patch(target, patches):
    rows = target.shape[0]
    block = 128
    blocks = rows // block
    onehot = (target[:, None] == jnp.arange(patches, dtype=jnp.int32)[None, :]).astype(jnp.bfloat16)
    onehot = onehot.reshape(blocks, block, patches)
    lower = (jnp.arange(block)[:, None] >= jnp.arange(block)[None, :]).astype(jnp.bfloat16)
    within = jnp.einsum("ij,bjp->bip", lower, onehot, preferred_element_type=jnp.float32)
    totals = jnp.sum(onehot.astype(jnp.float32), 1)
    earlier = (jnp.arange(blocks)[:, None] > jnp.arange(blocks)[None, :]).astype(jnp.float32)
    before = jnp.dot(earlier, totals, precision=HIGHEST)
    count = jnp.sum((within + before[:, None, :]) * onehot.astype(jnp.float32), 2)
    return count.reshape(rows).astype(jnp.int32) - 1


def per_device(background, evolved, obs_value, obs_var, obs_patch, obs_pos):
    mem_count = lax.axis_size("mem")
    tile_count = lax.axis_size("tile")
    patches = mem_count * tile_count
    local_members = evolved.shape[0]
    members = local_members * mem_count
    slot_count = 2 * OBS_PATCH
    capacity = slot_count // tile_count
    cells = background.shape[3]

    states = lax.all_to_all(background, "mem", split_axis=1, concat_axis=0, tiled=True)
    flat_states = states.reshape(members, cells)
    state_sum = jnp.sum(flat_states.astype(jnp.float32), 0)
    state_mean = state_sum / members
    deviation = (flat_states.astype(jnp.float32) - state_mean[None, :]).astype(jnp.bfloat16)

    target = obs_patch[:, 0]
    slot_rank = rank_in_patch(target, patches)
    slot_place = target * capacity + slot_rank
    rows = jnp.concatenate(
        [evolved, jnp.stack([obs_value, obs_var, (obs_pos + 1).astype(jnp.bfloat16)])], 0
    )
    send = jnp.zeros((rows.shape[0], patches * capacity), jnp.bfloat16).at[:, slot_place].set(rows)
    send = send.reshape(rows.shape[0], patches, capacity).transpose(1, 0, 2)
    got = lax.all_to_all(send, ("mem", "tile"), split_axis=0, concat_axis=0, tiled=True)
    axis = ("mem", "tile")
    mats, vecs = partial_grams(got, mem_count, tile_count, local_members)
    next_mat, own_mat, prev_mat = mats[0], mats[1], mats[2]
    next_vec, own_vec, prev_vec = vecs[0], vecs[1], vecs[2]
    diag_mask = jnp.eye(members, dtype=jnp.bool_)
    from_prev = ring_shift(next_mat.astype(jnp.bfloat16), axis, 1)
    from_prev_side = ring_shift(jnp.stack([next_vec, jnp.sum(jnp.where(diag_mask, next_mat, 0.0), 0)]), axis, 1)
    from_next = ring_shift(prev_mat.astype(jnp.bfloat16), axis, -1)
    from_next_side = ring_shift(jnp.stack([prev_vec, jnp.sum(jnp.where(diag_mask, prev_mat, 0.0), 0)]), axis, -1)
    from_prev = jnp.where(diag_mask, from_prev_side[1][None, :], from_prev.astype(jnp.float32))
    from_next = jnp.where(diag_mask, from_next_side[1][None, :], from_next.astype(jnp.float32))
    gram_mat = own_mat + from_prev + from_next
    gram_vec = own_vec + from_prev_side[0] + from_next_side[0]
    transform_mat = transform(gram_mat, gram_vec)

    mixed = lax.dot_general(
        transform_mat, deviation, (((0,), (0,)), ((), ())), preferred_element_type=jnp.float32
    )
    updated = (state_mean[None, :] + mixed).astype(jnp.bfloat16)
    chunks = updated.reshape(mem_count, local_members, cells)
    me = lax.axis_index("mem")
    back = jnp.zeros((local_members, mem_count, cells), jnp.bfloat16)
    for shift in range(mem_count):
        piece = lax.dynamic_index_in_dim(chunks, (me + shift) % mem_count, 0, keepdims=False)
        if shift:
            pairs = [(i, (i + shift) % mem_count) for i in range(mem_count)]
            piece = lax.ppermute(piece, "mem", pairs)
        source = (me - shift) % mem_count
        back = lax.dynamic_update_slice(back, piece[:, None, :], (0, source, 0))
    return back.reshape(local_members, mem_count, 1, cells)


def solution(mesh):
    return jax.shard_map(
        per_device,
        mesh=mesh,
        in_specs=(
            P("mem", None, "tile", None),
            P("mem", "tile"),
            P("tile"),
            P("tile"),
            P("tile", None),
            P("tile"),
        ),
        out_specs=P("mem", None, "tile", None),
        check_vma=False,
    )
```

```python
import functools
import math

import jax
import jax.numpy as jnp
from jax import lax
from jax.experimental import pallas as pl
from jax.sharding import PartitionSpec as P

PATCH_CELLS = 128
OBS_PATCH = 1024
ITERS = 4
HIGHEST = lax.Precision.HIGHEST
NEWTON = lax.Precision.HIGH


def ring_shift(block, axis, step):
    count = 1
    for name in axis:
        count *= lax.axis_size(name)
    pairs = [(i, (i + step) % count) for i in range(count)]
    return lax.ppermute(block, axis, pairs)


def localize(position, offset):
    distance = (offset * PATCH_CELLS + position + 0.5 - 0.5 * PATCH_CELLS) / PATCH_CELLS
    return jnp.exp(-2.0 * distance * distance)


def obs_weight(var_row, shifted_row):
    is_live = shifted_row.astype(jnp.float32) > 0.5
    safe_var = jnp.where(is_live, var_row.astype(jnp.float32), 1.0)
    return (jnp.where(is_live, 1.0 / safe_var, 0.0), shifted_row.astype(jnp.float32) - 1.0)


def block_terms(block, members, offset):
    centred = block[:members]
    innovation = block[members]
    weight, position = obs_weight(block[members + 1], block[members + 2])
    scale = weight * localize(position, offset)
    weighted = (centred.astype(jnp.float32) * scale[None, :]).astype(jnp.bfloat16)
    gram_mat = lax.dot_general(
        weighted, centred, (((1,), (1,)), ((), ())), preferred_element_type=jnp.float32
    )
    gram_vec = jnp.dot(weighted, innovation, preferred_element_type=jnp.float32)
    return gram_mat, gram_vec


def gram_kernel(x_ref, mat_ref, vec_ref, low_ref, *, local_members, mem_count, tiles_per_step):
    step = pl.program_id(0)

    @pl.when(step == 0)
    def _():
        mat_ref[...] = jnp.zeros_like(mat_ref)
        vec_ref[...] = jnp.zeros_like(vec_ref)

    members = local_members * mem_count
    block = x_ref[...]
    slots = block.shape[-1]
    values = jnp.concatenate(
        [block[:, j, :local_members, :].reshape(members, slots) for j in range(tiles_per_step)], 1
    ).astype(jnp.float32)
    info = jnp.concatenate(
        [block[0, j, local_members:local_members + 3, :] for j in range(tiles_per_step)], 1
    ).astype(jnp.float32)
    obs_mean = jnp.sum(values, 0, keepdims=True) / members
    centred = (values - obs_mean).astype(jnp.bfloat16)
    innovation = (info[0:1] - obs_mean).astype(jnp.bfloat16)
    is_live = info[2:3] > 0.5
    weight = jnp.where(is_live, 1.0 / jnp.where(is_live, info[1:2], 1.0), 0.0)
    position = info[2:3] - 1.0
    centred_f = centred.astype(jnp.float32)
    weighted = jnp.concatenate(
        [
            (centred_f * (weight * localize(position, offset))).astype(jnp.bfloat16)
            for offset in (-1.0, 0.0, 1.0)
        ],
        0,
    )
    mat_ref[...] += lax.dot_general(
        weighted, centred, (((1,), (1,)), ((), ())), preferred_element_type=jnp.float32
    )
    innov_rows = jnp.broadcast_to(innovation, (8, innovation.shape[1]))
    vec_ref[...] += lax.dot_general(
        innov_rows, weighted, (((1,), (1,)), ((), ())), preferred_element_type=jnp.float32
    )

    @pl.when(step == pl.num_programs(0) - 1)
    def _():
        diag_mask = (
            lax.broadcasted_iota(jnp.int32, (members, members), 0)
            == lax.broadcasted_iota(jnp.int32, (members, members), 1)
        )
        for index, part in enumerate((0, 2)):
            mat = mat_ref[part * members:(part + 1) * members, :]
            low_ref[index] = mat.astype(jnp.bfloat16)
            vec_ref[1:2, part * members:(part + 1) * members] = jnp.sum(
                jnp.where(diag_mask, mat, 0.0), 0, keepdims=True
            )


def partial_grams(received, mem_count, tile_count, local_members):
    rows, slots = received.shape[1], received.shape[2]
    members = local_members * mem_count
    tiles_per_step = 2
    x = received.reshape(mem_count, tile_count, rows, slots)
    kernel = functools.partial(
        gram_kernel, local_members=local_members, mem_count=mem_count, tiles_per_step=tiles_per_step
    )
    mat, vec, low = pl.pallas_call(
        kernel,
        grid=(tile_count // tiles_per_step,),
        in_specs=[pl.BlockSpec((mem_count, tiles_per_step, rows, slots), lambda t: (0, t, 0, 0))],
        out_specs=[
            pl.BlockSpec((3 * members, members), lambda t: (0, 0)),
            pl.BlockSpec((8, 3 * members), lambda t: (0, 0)),
            pl.BlockSpec((2, members, members), lambda t: (0, 0, 0)),
        ],
        out_shape=[
            jax.ShapeDtypeStruct((3 * members, members), jnp.float32),
            jax.ShapeDtypeStruct((8, 3 * members), jnp.float32),
            jax.ShapeDtypeStruct((2, members, members), jnp.bfloat16),
        ],
    )(x)
    return mat.reshape(3, members, members), vec[:2].reshape(2, 3, members), low


def inverse_root(gram_mat):
    mat_size = gram_mat.shape[0]
    identity = jnp.eye(mat_size, dtype=jnp.float32)
    norm_scale = jnp.sqrt(jnp.sum(gram_mat * gram_mat))
    root_up = gram_mat / norm_scale
    root_down = None
    for sweep_index in range(ITERS):
        if root_down is None:
            product = root_up
        else:
            product = jnp.dot(root_down, root_up, precision=NEWTON)
        middle = 1.5 * identity - 0.5 * product
        if sweep_index + 1 < ITERS:
            root_up = jnp.dot(root_up, middle, precision=NEWTON)
        root_down = middle if root_down is None else jnp.dot(middle, root_down, precision=NEWTON)
    return root_down / jnp.sqrt(norm_scale)


def transform(gram_mat, gram_vec):
    mat_size = gram_mat.shape[0]
    identity = jnp.eye(mat_size, dtype=jnp.float32)
    inv_root = inverse_root(gram_mat + (mat_size - 1.0) * identity)
    inner_w = jnp.dot(inv_root, gram_vec, precision=HIGHEST)
    mean_w = jnp.dot(inv_root, inner_w, precision=HIGHEST)
    return (math.sqrt(mat_size - 1.0) * inv_root + mean_w[:, None]).astype(jnp.bfloat16)


def rank_in_patch(target, patches):
    rows = target.shape[0]
    block = 128
    blocks = rows // block
    onehot = (target[:, None] == jnp.arange(patches, dtype=jnp.int32)[None, :]).astype(jnp.bfloat16)
    onehot = onehot.reshape(blocks, block, patches)
    lower = (jnp.arange(block)[:, None] >= jnp.arange(block)[None, :]).astype(jnp.bfloat16)
    within = jnp.einsum("ij,bjp->bip", lower, onehot, preferred_element_type=jnp.float32)
    totals = jnp.sum(onehot.astype(jnp.float32), 1)
    earlier = (jnp.arange(blocks)[:, None] > jnp.arange(blocks)[None, :]).astype(jnp.float32)
    before = jnp.dot(earlier, totals, precision=HIGHEST)
    count = jnp.sum((within + before[:, None, :]) * onehot.astype(jnp.float32), 2)
    return count.reshape(rows).astype(jnp.int32) - 1


def per_device(background, evolved, obs_value, obs_var, obs_patch, obs_pos):
    mem_count = lax.axis_size("mem")
    tile_count = lax.axis_size("tile")
    patches = mem_count * tile_count
    local_members = evolved.shape[0]
    members = local_members * mem_count
    slot_count = 2 * OBS_PATCH
    capacity = slot_count // tile_count
    cells = background.shape[3]

    states = lax.all_to_all(background, "mem", split_axis=1, concat_axis=0, tiled=True)
    flat_states = states.reshape(members, cells)
    state_sum = jnp.sum(flat_states.astype(jnp.float32), 0)
    state_mean = state_sum / members
    deviation = (flat_states.astype(jnp.float32) - state_mean[None, :]).astype(jnp.bfloat16)

    target = obs_patch[:, 0]
    slot_rank = rank_in_patch(target, patches)
    slot_place = target * capacity + slot_rank
    rows = jnp.concatenate(
        [evolved, jnp.stack([obs_value, obs_var, (obs_pos + 1).astype(jnp.bfloat16)])], 0
    )
    send = jnp.zeros((rows.shape[0], patches * capacity), jnp.bfloat16).at[:, slot_place].set(rows)
    send = send.reshape(rows.shape[0], patches, capacity).transpose(1, 0, 2)
    got = lax.all_to_all(send, ("mem", "tile"), split_axis=0, concat_axis=0, tiled=True)
    axis = ("mem", "tile")
    mats, sides, low = partial_grams(got, mem_count, tile_count, local_members)
    own_mat = mats[1]
    own_vec = sides[0, 1]
    diag_mask = jnp.eye(members, dtype=jnp.bool_)
    from_prev = ring_shift(low[0], axis, 1)
    from_prev_side = ring_shift(sides[:, 0], axis, 1)
    from_next = ring_shift(low[1], axis, -1)
    from_next_side = ring_shift(sides[:, 2], axis, -1)
    from_prev = jnp.where(diag_mask, from_prev_side[1][None, :], from_prev.astype(jnp.float32))
    from_next = jnp.where(diag_mask, from_next_side[1][None, :], from_next.astype(jnp.float32))
    gram_mat = own_mat + from_prev + from_next
    gram_vec = own_vec + from_prev_side[0] + from_next_side[0]
    transform_mat = transform(gram_mat, gram_vec)

    mixed = lax.dot_general(
        transform_mat, deviation, (((0,), (0,)), ((), ())), preferred_element_type=jnp.float32
    )
    updated = (state_mean[None, :] + mixed).astype(jnp.bfloat16)
    chunks = updated.reshape(mem_count, local_members, cells)
    me = lax.axis_index("mem")
    pieces = []
    for shift in range(mem_count):
        piece = lax.dynamic_index_in_dim(chunks, (me + shift) % mem_count, 0, keepdims=False)
        if shift:
            pairs = [(i, (i + shift) % mem_count) for i in range(mem_count)]
            piece = lax.ppermute(piece, "mem", pairs)
        pieces.append(piece)
    by_shift = jnp.stack(pieces)
    back = jnp.take(by_shift, (me - jnp.arange(mem_count)) % mem_count, axis=0)
    return back.transpose(1, 0, 2).reshape(local_members, mem_count, 1, cells)


def solution(mesh):
    return jax.shard_map(
        per_device,
        mesh=mesh,
        in_specs=(
            P("mem", None, "tile", None),
            P("mem", "tile"),
            P("tile"),
            P("tile"),
            P("tile", None),
            P("tile"),
        ),
        out_specs=P("mem", None, "tile", None),
        check_vma=False,
    )
```

```python
import functools
import math

import jax
import jax.numpy as jnp
from jax import lax
from jax.experimental import pallas as pl
from jax.sharding import PartitionSpec as P

PATCH_CELLS = 128
OBS_PATCH = 1024
ITERS = 4
HIGHEST = lax.Precision.HIGHEST
NEWTON = lax.Precision.HIGH


def ring_shift(block, axis, step):
    count = 1
    for name in axis:
        count *= lax.axis_size(name)
    pairs = [(i, (i + step) % count) for i in range(count)]
    return lax.ppermute(block, axis, pairs)


def localize(position, offset):
    distance = (offset * PATCH_CELLS + position + 0.5 - 0.5 * PATCH_CELLS) / PATCH_CELLS
    return jnp.exp(-2.0 * distance * distance)


def obs_weight(var_row, shifted_row):
    is_live = shifted_row.astype(jnp.float32) > 0.5
    safe_var = jnp.where(is_live, var_row.astype(jnp.float32), 1.0)
    return (jnp.where(is_live, 1.0 / safe_var, 0.0), shifted_row.astype(jnp.float32) - 1.0)


def block_terms(block, members, offset):
    centred = block[:members]
    innovation = block[members]
    weight, position = obs_weight(block[members + 1], block[members + 2])
    scale = weight * localize(position, offset)
    weighted = (centred.astype(jnp.float32) * scale[None, :]).astype(jnp.bfloat16)
    gram_mat = lax.dot_general(
        weighted, centred, (((1,), (1,)), ((), ())), preferred_element_type=jnp.float32
    )
    gram_vec = jnp.dot(weighted, innovation, preferred_element_type=jnp.float32)
    return gram_mat, gram_vec


def gram_kernel(x_ref, mat_ref, vec_ref, low_ref, *, local_members, mem_count, tiles_per_step):
    step = pl.program_id(0)

    @pl.when(step == 0)
    def _():
        mat_ref[...] = jnp.zeros_like(mat_ref)
        vec_ref[...] = jnp.zeros_like(vec_ref)

    members = local_members * mem_count
    block = x_ref[...]
    slots = block.shape[-1]
    values = jnp.concatenate(
        [block[:, j, :local_members, :].reshape(members, slots) for j in range(tiles_per_step)], 1
    ).astype(jnp.float32)
    info = jnp.concatenate(
        [block[0, j, local_members:local_members + 3, :] for j in range(tiles_per_step)], 1
    ).astype(jnp.float32)
    obs_mean = jnp.sum(values, 0, keepdims=True) / members
    centred = (values - obs_mean).astype(jnp.bfloat16)
    innovation = (info[0:1] - obs_mean).astype(jnp.bfloat16)
    is_live = info[2:3] > 0.5
    weight = jnp.where(is_live, 1.0 / jnp.where(is_live, info[1:2], 1.0), 0.0)
    position = info[2:3] - 1.0
    centred_f = centred.astype(jnp.float32)
    weighted = jnp.concatenate(
        [
            (centred_f * (weight * localize(position, offset))).astype(jnp.bfloat16)
            for offset in (-1.0, 0.0, 1.0)
        ],
        0,
    )
    mat_ref[...] += lax.dot_general(
        weighted, centred, (((1,), (1,)), ((), ())), preferred_element_type=jnp.float32
    )
    innov_rows = jnp.broadcast_to(innovation, (8, innovation.shape[1]))
    vec_ref[...] += lax.dot_general(
        innov_rows, weighted, (((1,), (1,)), ((), ())), preferred_element_type=jnp.float32
    )

    @pl.when(step == pl.num_programs(0) - 1)
    def _():
        diag_mask = (
            lax.broadcasted_iota(jnp.int32, (members, members), 0)
            == lax.broadcasted_iota(jnp.int32, (members, members), 1)
        )
        for index, part in enumerate((0, 2)):
            mat = mat_ref[part * members:(part + 1) * members, :]
            low_ref[index] = mat.astype(jnp.bfloat16)
            vec_ref[1:2, part * members:(part + 1) * members] = jnp.sum(
                jnp.where(diag_mask, mat, 0.0), 0, keepdims=True
            )


def partial_grams(received, mem_count, tile_count, local_members):
    rows, slots = received.shape[1], received.shape[2]
    members = local_members * mem_count
    tiles_per_step = 2
    x = received.reshape(mem_count, tile_count, rows, slots)
    kernel = functools.partial(
        gram_kernel, local_members=local_members, mem_count=mem_count, tiles_per_step=tiles_per_step
    )
    mat, vec, low = pl.pallas_call(
        kernel,
        grid=(tile_count // tiles_per_step,),
        in_specs=[pl.BlockSpec((mem_count, tiles_per_step, rows, slots), lambda t: (0, t, 0, 0))],
        out_specs=[
            pl.BlockSpec((3 * members, members), lambda t: (0, 0)),
            pl.BlockSpec((8, 3 * members), lambda t: (0, 0)),
            pl.BlockSpec((2, members, members), lambda t: (0, 0, 0)),
        ],
        out_shape=[
            jax.ShapeDtypeStruct((3 * members, members), jnp.float32),
            jax.ShapeDtypeStruct((8, 3 * members), jnp.float32),
            jax.ShapeDtypeStruct((2, members, members), jnp.bfloat16),
        ],
    )(x)
    return mat.reshape(3, members, members), vec[:2].reshape(2, 3, members), low


def inverse_root(gram_mat):
    mat_size = gram_mat.shape[0]
    identity = jnp.eye(mat_size, dtype=jnp.float32)
    norm_scale = jnp.sqrt(jnp.sum(gram_mat * gram_mat))
    root_up = gram_mat / norm_scale
    root_down = None
    for sweep_index in range(ITERS):
        if root_down is None:
            product = root_up
        else:
            product = jnp.dot(root_down, root_up, precision=NEWTON)
        middle = 1.5 * identity - 0.5 * product
        if sweep_index + 1 < ITERS:
            root_up = jnp.dot(root_up, middle, precision=NEWTON)
        root_down = middle if root_down is None else jnp.dot(middle, root_down, precision=NEWTON)
    return root_down / jnp.sqrt(norm_scale)


def transform(gram_mat, gram_vec):
    mat_size = gram_mat.shape[0]
    identity = jnp.eye(mat_size, dtype=jnp.float32)
    inv_root = inverse_root(gram_mat + (mat_size - 1.0) * identity)
    inner_w = jnp.dot(inv_root, gram_vec, precision=NEWTON)
    mean_w = jnp.dot(inv_root, inner_w, precision=NEWTON)
    return (math.sqrt(mat_size - 1.0) * inv_root + mean_w[:, None]).astype(jnp.bfloat16)


def rank_in_patch(target, patches):
    rows = target.shape[0]
    block = 128
    blocks = rows // block
    onehot = (target[:, None] == jnp.arange(patches, dtype=jnp.int32)[None, :]).astype(jnp.bfloat16)
    onehot = onehot.reshape(blocks, block, patches)
    lower = (jnp.arange(block)[:, None] >= jnp.arange(block)[None, :]).astype(jnp.bfloat16)
    within = jnp.einsum("ij,bjp->bip", lower, onehot, preferred_element_type=jnp.float32)
    totals = jnp.sum(onehot.astype(jnp.float32), 1)
    earlier = (jnp.arange(blocks)[:, None] > jnp.arange(blocks)[None, :]).astype(jnp.float32)
    before = jnp.dot(earlier, totals, precision=HIGHEST)
    count = jnp.sum((within + before[:, None, :]) * onehot.astype(jnp.float32), 2)
    return count.reshape(rows).astype(jnp.int32) - 1


def per_device(background, evolved, obs_value, obs_var, obs_patch, obs_pos):
    mem_count = lax.axis_size("mem")
    tile_count = lax.axis_size("tile")
    patches = mem_count * tile_count
    local_members = evolved.shape[0]
    members = local_members * mem_count
    slot_count = 2 * OBS_PATCH
    capacity = slot_count // tile_count
    cells = background.shape[3]

    states = lax.all_to_all(background, "mem", split_axis=1, concat_axis=0, tiled=True)
    flat_states = states.reshape(members, cells)
    state_sum = jnp.sum(flat_states.astype(jnp.float32), 0)
    state_mean = state_sum / members
    deviation = (flat_states.astype(jnp.float32) - state_mean[None, :]).astype(jnp.bfloat16)

    target = obs_patch[:, 0]
    slot_rank = rank_in_patch(target, patches)
    slot_place = target * capacity + slot_rank
    rows = jnp.concatenate(
        [evolved, jnp.stack([obs_value, obs_var, (obs_pos + 1).astype(jnp.bfloat16)])], 0
    )
    send = jnp.zeros((rows.shape[0], patches * capacity), jnp.bfloat16).at[:, slot_place].set(rows)
    send = send.reshape(rows.shape[0], patches, capacity).transpose(1, 0, 2)
    got = lax.all_to_all(send, ("mem", "tile"), split_axis=0, concat_axis=0, tiled=True)
    axis = ("mem", "tile")
    mats, sides, low = partial_grams(got, mem_count, tile_count, local_members)
    own_mat = mats[1]
    own_vec = sides[0, 1]
    diag_mask = jnp.eye(members, dtype=jnp.bool_)
    from_prev = ring_shift(low[0], axis, 1)
    from_prev_side = ring_shift(sides[:, 0], axis, 1)
    from_next = ring_shift(low[1], axis, -1)
    from_next_side = ring_shift(sides[:, 2], axis, -1)
    from_prev = jnp.where(diag_mask, from_prev_side[1][None, :], from_prev.astype(jnp.float32))
    from_next = jnp.where(diag_mask, from_next_side[1][None, :], from_next.astype(jnp.float32))
    gram_mat = own_mat + from_prev + from_next
    gram_vec = own_vec + from_prev_side[0] + from_next_side[0]
    transform_mat = transform(gram_mat, gram_vec)

    mixed = lax.dot_general(
        transform_mat, deviation, (((0,), (0,)), ((), ())), preferred_element_type=jnp.float32
    )
    updated = (state_mean[None, :] + mixed).astype(jnp.bfloat16)
    chunks = updated.reshape(mem_count, local_members, cells)
    me = lax.axis_index("mem")
    pieces = []
    for shift in range(mem_count):
        piece = lax.dynamic_index_in_dim(chunks, (me + shift) % mem_count, 0, keepdims=False)
        if shift:
            pairs = [(i, (i + shift) % mem_count) for i in range(mem_count)]
            piece = lax.ppermute(piece, "mem", pairs)
        pieces.append(piece)
    by_shift = jnp.stack(pieces)
    back = jnp.take(by_shift, (me - jnp.arange(mem_count)) % mem_count, axis=0)
    return back.transpose(1, 0, 2).reshape(local_members, mem_count, 1, cells)


def solution(mesh):
    return jax.shard_map(
        per_device,
        mesh=mesh,
        in_specs=(
            P("mem", None, "tile", None),
            P("mem", "tile"),
            P("tile"),
            P("tile"),
            P("tile", None),
            P("tile"),
        ),
        out_specs=P("mem", None, "tile", None),
        check_vma=False,
    )
```

```python
import functools
import math

import jax
import jax.numpy as jnp
from jax import lax
from jax.experimental import pallas as pl
from jax.sharding import PartitionSpec as P

PATCH_CELLS = 128
OBS_PATCH = 1024
ITERS = 4
HIGHEST = lax.Precision.HIGHEST
NEWTON = lax.Precision.HIGH


def ring_shift(block, axis, step):
    count = 1
    for name in axis:
        count *= lax.axis_size(name)
    pairs = [(i, (i + step) % count) for i in range(count)]
    return lax.ppermute(block, axis, pairs)


def localize(position, offset):
    distance = (offset * PATCH_CELLS + position + 0.5 - 0.5 * PATCH_CELLS) / PATCH_CELLS
    return jnp.exp(-2.0 * distance * distance)


def obs_weight(var_row, shifted_row):
    is_live = shifted_row.astype(jnp.float32) > 0.5
    safe_var = jnp.where(is_live, var_row.astype(jnp.float32), 1.0)
    return (jnp.where(is_live, 1.0 / safe_var, 0.0), shifted_row.astype(jnp.float32) - 1.0)


def block_terms(block, members, offset):
    centred = block[:members]
    innovation = block[members]
    weight, position = obs_weight(block[members + 1], block[members + 2])
    scale = weight * localize(position, offset)
    weighted = (centred.astype(jnp.float32) * scale[None, :]).astype(jnp.bfloat16)
    gram_mat = lax.dot_general(
        weighted, centred, (((1,), (1,)), ((), ())), preferred_element_type=jnp.float32
    )
    gram_vec = jnp.dot(weighted, innovation, preferred_element_type=jnp.float32)
    return gram_mat, gram_vec


def gram_kernel(x_ref, mat_ref, vec_ref, low_ref, *, local_members, mem_count, tiles_per_step):
    step = pl.program_id(0)

    @pl.when(step == 0)
    def _():
        mat_ref[...] = jnp.zeros_like(mat_ref)
        vec_ref[...] = jnp.zeros_like(vec_ref)

    members = local_members * mem_count
    block = x_ref[...]
    slots = block.shape[-1]
    values = jnp.concatenate(
        [block[:, j, :local_members, :].reshape(members, slots) for j in range(tiles_per_step)], 1
    ).astype(jnp.float32)
    info = jnp.concatenate(
        [block[0, j, local_members:local_members + 3, :] for j in range(tiles_per_step)], 1
    ).astype(jnp.float32)
    obs_mean = jnp.sum(values, 0, keepdims=True) / members
    centred = (values - obs_mean).astype(jnp.bfloat16)
    innovation = (info[0:1] - obs_mean).astype(jnp.bfloat16)
    is_live = info[2:3] > 0.5
    weight = jnp.where(is_live, 1.0 / jnp.where(is_live, info[1:2], 1.0), 0.0)
    position = info[2:3] - 1.0
    centred_f = centred.astype(jnp.float32)
    weighted = jnp.concatenate(
        [
            (centred_f * (weight * localize(position, offset))).astype(jnp.bfloat16)
            for offset in (-1.0, 0.0, 1.0)
        ],
        0,
    )
    mat_ref[...] += lax.dot_general(
        weighted, centred, (((1,), (1,)), ((), ())), preferred_element_type=jnp.float32
    )
    innov_rows = jnp.broadcast_to(innovation, (8, innovation.shape[1]))
    vec_ref[...] += lax.dot_general(
        innov_rows, weighted, (((1,), (1,)), ((), ())), preferred_element_type=jnp.float32
    )

    @pl.when(step == pl.num_programs(0) - 1)
    def _():
        diag_mask = (
            lax.broadcasted_iota(jnp.int32, (members, members), 0)
            == lax.broadcasted_iota(jnp.int32, (members, members), 1)
        )
        for index, part in enumerate((0, 2)):
            mat = mat_ref[part * members:(part + 1) * members, :]
            low_ref[index] = mat.astype(jnp.bfloat16)
            vec_ref[1:2, part * members:(part + 1) * members] = jnp.sum(
                jnp.where(diag_mask, mat, 0.0), 0, keepdims=True
            )


def partial_grams(received, mem_count, tile_count, local_members):
    rows, slots = received.shape[1], received.shape[2]
    members = local_members * mem_count
    tiles_per_step = 4
    x = received.reshape(mem_count, tile_count, rows, slots)
    kernel = functools.partial(
        gram_kernel, local_members=local_members, mem_count=mem_count, tiles_per_step=tiles_per_step
    )
    mat, vec, low = pl.pallas_call(
        kernel,
        grid=(tile_count // tiles_per_step,),
        in_specs=[pl.BlockSpec((mem_count, tiles_per_step, rows, slots), lambda t: (0, t, 0, 0))],
        out_specs=[
            pl.BlockSpec((3 * members, members), lambda t: (0, 0)),
            pl.BlockSpec((8, 3 * members), lambda t: (0, 0)),
            pl.BlockSpec((2, members, members), lambda t: (0, 0, 0)),
        ],
        out_shape=[
            jax.ShapeDtypeStruct((3 * members, members), jnp.float32),
            jax.ShapeDtypeStruct((8, 3 * members), jnp.float32),
            jax.ShapeDtypeStruct((2, members, members), jnp.bfloat16),
        ],
    )(x)
    return mat.reshape(3, members, members), vec[:2].reshape(2, 3, members), low


def inverse_root(gram_mat):
    mat_size = gram_mat.shape[0]
    identity = jnp.eye(mat_size, dtype=jnp.float32)
    norm_scale = jnp.sqrt(jnp.sum(gram_mat * gram_mat))
    root_up = gram_mat / norm_scale
    root_down = None
    for sweep_index in range(ITERS):
        if root_down is None:
            product = root_up
        else:
            product = jnp.dot(root_down, root_up, precision=NEWTON)
        middle = 1.5 * identity - 0.5 * product
        if sweep_index + 1 < ITERS:
            root_up = jnp.dot(root_up, middle, precision=NEWTON)
        root_down = middle if root_down is None else jnp.dot(middle, root_down, precision=NEWTON)
    return root_down / jnp.sqrt(norm_scale)


def transform(gram_mat, gram_vec):
    mat_size = gram_mat.shape[0]
    identity = jnp.eye(mat_size, dtype=jnp.float32)
    inv_root = inverse_root(gram_mat + (mat_size - 1.0) * identity)
    inner_w = jnp.dot(inv_root, gram_vec, precision=NEWTON)
    mean_w = jnp.dot(inv_root, inner_w, precision=NEWTON)
    return (math.sqrt(mat_size - 1.0) * inv_root + mean_w[:, None]).astype(jnp.bfloat16)


def rank_in_patch(target, patches):
    rows = target.shape[0]
    block = 128
    blocks = rows // block
    onehot = (target[:, None] == jnp.arange(patches, dtype=jnp.int32)[None, :]).astype(jnp.bfloat16)
    onehot = onehot.reshape(blocks, block, patches)
    lower = (jnp.arange(block)[:, None] >= jnp.arange(block)[None, :]).astype(jnp.bfloat16)
    within = jnp.einsum("ij,bjp->bip", lower, onehot, preferred_element_type=jnp.float32)
    totals = jnp.sum(onehot.astype(jnp.float32), 1)
    earlier = (jnp.arange(blocks)[:, None] > jnp.arange(blocks)[None, :]).astype(jnp.float32)
    before = jnp.dot(earlier, totals, precision=HIGHEST)
    count = jnp.sum((within + before[:, None, :]) * onehot.astype(jnp.float32), 2)
    return count.reshape(rows).astype(jnp.int32) - 1


def per_device(background, evolved, obs_value, obs_var, obs_patch, obs_pos):
    mem_count = lax.axis_size("mem")
    tile_count = lax.axis_size("tile")
    patches = mem_count * tile_count
    local_members = evolved.shape[0]
    members = local_members * mem_count
    slot_count = 2 * OBS_PATCH
    capacity = slot_count // tile_count
    cells = background.shape[3]

    states = lax.all_to_all(background, "mem", split_axis=1, concat_axis=0, tiled=True)
    flat_states = states.reshape(members, cells)
    state_sum = jnp.sum(flat_states.astype(jnp.float32), 0)
    state_mean = state_sum / members
    deviation = (flat_states.astype(jnp.float32) - state_mean[None, :]).astype(jnp.bfloat16)

    target = obs_patch[:, 0]
    slot_rank = rank_in_patch(target, patches)
    slot_place = target * capacity + slot_rank
    rows = jnp.concatenate(
        [evolved, jnp.stack([obs_value, obs_var, (obs_pos + 1).astype(jnp.bfloat16)])], 0
    )
    send = jnp.zeros((rows.shape[0], patches * capacity), jnp.bfloat16).at[:, slot_place].set(rows)
    send = send.reshape(rows.shape[0], patches, capacity).transpose(1, 0, 2)
    got = lax.all_to_all(send, ("mem", "tile"), split_axis=0, concat_axis=0, tiled=True)
    axis = ("mem", "tile")
    mats, sides, low = partial_grams(got, mem_count, tile_count, local_members)
    own_mat = mats[1]
    own_vec = sides[0, 1]
    diag_mask = jnp.eye(members, dtype=jnp.bool_)
    from_prev = ring_shift(low[0], axis, 1)
    from_prev_side = ring_shift(sides[:, 0], axis, 1)
    from_next = ring_shift(low[1], axis, -1)
    from_next_side = ring_shift(sides[:, 2], axis, -1)
    from_prev = jnp.where(diag_mask, from_prev_side[1][None, :], from_prev.astype(jnp.float32))
    from_next = jnp.where(diag_mask, from_next_side[1][None, :], from_next.astype(jnp.float32))
    gram_mat = own_mat + from_prev + from_next
    gram_vec = own_vec + from_prev_side[0] + from_next_side[0]
    transform_mat = transform(gram_mat, gram_vec)

    mixed = lax.dot_general(
        transform_mat, deviation, (((0,), (0,)), ((), ())), preferred_element_type=jnp.float32
    )
    updated = (state_mean[None, :] + mixed).astype(jnp.bfloat16)
    chunks = updated.reshape(mem_count, local_members, cells)
    me = lax.axis_index("mem")
    pieces = []
    for shift in range(mem_count):
        piece = lax.dynamic_index_in_dim(chunks, (me + shift) % mem_count, 0, keepdims=False)
        if shift:
            pairs = [(i, (i + shift) % mem_count) for i in range(mem_count)]
            piece = lax.ppermute(piece, "mem", pairs)
        pieces.append(piece)
    by_shift = jnp.stack(pieces)
    back = jnp.take(by_shift, (me - jnp.arange(mem_count)) % mem_count, axis=0)
    return back.transpose(1, 0, 2).reshape(local_members, mem_count, 1, cells)


def solution(mesh):
    return jax.shard_map(
        per_device,
        mesh=mesh,
        in_specs=(
            P("mem", None, "tile", None),
            P("mem", "tile"),
            P("tile"),
            P("tile"),
            P("tile", None),
            P("tile"),
        ),
        out_specs=P("mem", None, "tile", None),
        check_vma=False,
    )
```

```python
import functools
import math

import jax
import jax.numpy as jnp
from jax import lax
from jax.experimental import pallas as pl
from jax.sharding import PartitionSpec as P

PATCH_CELLS = 128
OBS_PATCH = 1024
ITERS = 4
HIGHEST = lax.Precision.HIGHEST
NEWTON = lax.Precision.HIGH


def ring_shift(block, axis, step):
    count = 1
    for name in axis:
        count *= lax.axis_size(name)
    pairs = [(i, (i + step) % count) for i in range(count)]
    return lax.ppermute(block, axis, pairs)


def localize(position, offset):
    distance = (offset * PATCH_CELLS + position + 0.5 - 0.5 * PATCH_CELLS) / PATCH_CELLS
    return jnp.exp(-2.0 * distance * distance)


def obs_weight(var_row, shifted_row):
    is_live = shifted_row.astype(jnp.float32) > 0.5
    safe_var = jnp.where(is_live, var_row.astype(jnp.float32), 1.0)
    return (jnp.where(is_live, 1.0 / safe_var, 0.0), shifted_row.astype(jnp.float32) - 1.0)


def block_terms(block, members, offset):
    centred = block[:members]
    innovation = block[members]
    weight, position = obs_weight(block[members + 1], block[members + 2])
    scale = weight * localize(position, offset)
    weighted = (centred.astype(jnp.float32) * scale[None, :]).astype(jnp.bfloat16)
    gram_mat = lax.dot_general(
        weighted, centred, (((1,), (1,)), ((), ())), preferred_element_type=jnp.float32
    )
    gram_vec = jnp.dot(weighted, innovation, preferred_element_type=jnp.float32)
    return gram_mat, gram_vec


def gram_kernel(x_ref, mat_ref, vec_ref, low_ref, *, local_members, mem_count, tiles_per_step):
    step = pl.program_id(0)

    @pl.when(step == 0)
    def _():
        mat_ref[...] = jnp.zeros_like(mat_ref)
        vec_ref[...] = jnp.zeros_like(vec_ref)

    members = local_members * mem_count
    block = x_ref[...]
    slots = block.shape[-1]
    values = jnp.concatenate(
        [block[:, j, :local_members, :].reshape(members, slots) for j in range(tiles_per_step)], 1
    ).astype(jnp.float32)
    info = jnp.concatenate(
        [block[0, j, local_members:local_members + 3, :] for j in range(tiles_per_step)], 1
    ).astype(jnp.float32)
    obs_mean = jnp.sum(values, 0, keepdims=True) / members
    centred = (values - obs_mean).astype(jnp.bfloat16)
    innovation = (info[0:1] - obs_mean).astype(jnp.bfloat16)
    is_live = info[2:3] > 0.5
    weight = jnp.where(is_live, 1.0 / jnp.where(is_live, info[1:2], 1.0), 0.0)
    position = info[2:3] - 1.0
    centred_f = centred.astype(jnp.float32)
    weighted = jnp.concatenate(
        [
            (centred_f * (weight * localize(position, offset))).astype(jnp.bfloat16)
            for offset in (-1.0, 0.0, 1.0)
        ],
        0,
    )
    mat_ref[...] += lax.dot_general(
        weighted, centred, (((1,), (1,)), ((), ())), preferred_element_type=jnp.float32
    )
    innov_rows = jnp.broadcast_to(innovation, (8, innovation.shape[1]))
    vec_ref[...] += lax.dot_general(
        innov_rows, weighted, (((1,), (1,)), ((), ())), preferred_element_type=jnp.float32
    )

    @pl.when(step == pl.num_programs(0) - 1)
    def _():
        diag_mask = (
            lax.broadcasted_iota(jnp.int32, (members, members), 0)
            == lax.broadcasted_iota(jnp.int32, (members, members), 1)
        )
        for index, part in enumerate((0, 2)):
            mat = mat_ref[part * members:(part + 1) * members, :]
            low_ref[index] = mat.astype(jnp.bfloat16)
            vec_ref[1:2, part * members:(part + 1) * members] = jnp.sum(
                jnp.where(diag_mask, mat, 0.0), 0, keepdims=True
            )


def partial_grams(received, mem_count, tile_count, local_members):
    rows, slots = received.shape[1], received.shape[2]
    members = local_members * mem_count
    tiles_per_step = 8
    x = received.reshape(mem_count, tile_count, rows, slots)
    kernel = functools.partial(
        gram_kernel, local_members=local_members, mem_count=mem_count, tiles_per_step=tiles_per_step
    )
    mat, vec, low = pl.pallas_call(
        kernel,
        grid=(tile_count // tiles_per_step,),
        in_specs=[pl.BlockSpec((mem_count, tiles_per_step, rows, slots), lambda t: (0, t, 0, 0))],
        out_specs=[
            pl.BlockSpec((3 * members, members), lambda t: (0, 0)),
            pl.BlockSpec((8, 3 * members), lambda t: (0, 0)),
            pl.BlockSpec((2, members, members), lambda t: (0, 0, 0)),
        ],
        out_shape=[
            jax.ShapeDtypeStruct((3 * members, members), jnp.float32),
            jax.ShapeDtypeStruct((8, 3 * members), jnp.float32),
            jax.ShapeDtypeStruct((2, members, members), jnp.bfloat16),
        ],
    )(x)
    return mat.reshape(3, members, members), vec[:2].reshape(2, 3, members), low


def inverse_root(gram_mat):
    mat_size = gram_mat.shape[0]
    identity = jnp.eye(mat_size, dtype=jnp.float32)
    norm_scale = jnp.sqrt(jnp.sum(gram_mat * gram_mat))
    root_up = gram_mat / norm_scale
    root_down = None
    for sweep_index in range(ITERS):
        if root_down is None:
            product = root_up
        else:
            product = jnp.dot(root_down, root_up, precision=NEWTON)
        middle = 1.5 * identity - 0.5 * product
        if sweep_index + 1 < ITERS:
            root_up = jnp.dot(root_up, middle, precision=NEWTON)
        root_down = middle if root_down is None else jnp.dot(middle, root_down, precision=NEWTON)
    return root_down / jnp.sqrt(norm_scale)


def transform(gram_mat, gram_vec):
    mat_size = gram_mat.shape[0]
    identity = jnp.eye(mat_size, dtype=jnp.float32)
    inv_root = inverse_root(gram_mat + (mat_size - 1.0) * identity)
    inner_w = jnp.dot(inv_root, gram_vec, precision=NEWTON)
    mean_w = jnp.dot(inv_root, inner_w, precision=NEWTON)
    return (math.sqrt(mat_size - 1.0) * inv_root + mean_w[:, None]).astype(jnp.bfloat16)


def rank_in_patch(target, patches):
    rows = target.shape[0]
    block = 128
    blocks = rows // block
    onehot = (target[:, None] == jnp.arange(patches, dtype=jnp.int32)[None, :]).astype(jnp.bfloat16)
    onehot = onehot.reshape(blocks, block, patches)
    lower = (jnp.arange(block)[:, None] >= jnp.arange(block)[None, :]).astype(jnp.bfloat16)
    within = jnp.einsum("ij,bjp->bip", lower, onehot, preferred_element_type=jnp.float32)
    totals = jnp.sum(onehot.astype(jnp.float32), 1)
    earlier = (jnp.arange(blocks)[:, None] > jnp.arange(blocks)[None, :]).astype(jnp.float32)
    before = jnp.dot(earlier, totals, precision=HIGHEST)
    count = jnp.sum((within + before[:, None, :]) * onehot.astype(jnp.float32), 2)
    return count.reshape(rows).astype(jnp.int32) - 1


def per_device(background, evolved, obs_value, obs_var, obs_patch, obs_pos):
    mem_count = lax.axis_size("mem")
    tile_count = lax.axis_size("tile")
    patches = mem_count * tile_count
    local_members = evolved.shape[0]
    members = local_members * mem_count
    slot_count = 2 * OBS_PATCH
    capacity = slot_count // tile_count
    cells = background.shape[3]

    states = lax.all_to_all(background, "mem", split_axis=1, concat_axis=0, tiled=True)
    flat_states = states.reshape(members, cells)
    state_sum = jnp.sum(flat_states.astype(jnp.float32), 0)
    state_mean = state_sum / members
    deviation = (flat_states.astype(jnp.float32) - state_mean[None, :]).astype(jnp.bfloat16)

    target = obs_patch[:, 0]
    slot_rank = rank_in_patch(target, patches)
    slot_place = target * capacity + slot_rank
    rows = jnp.concatenate(
        [evolved, jnp.stack([obs_value, obs_var, (obs_pos + 1).astype(jnp.bfloat16)])], 0
    )
    send = jnp.zeros((rows.shape[0], patches * capacity), jnp.bfloat16).at[:, slot_place].set(rows)
    send = send.reshape(rows.shape[0], patches, capacity).transpose(1, 0, 2)
    got = lax.all_to_all(send, ("mem", "tile"), split_axis=0, concat_axis=0, tiled=True)
    axis = ("mem", "tile")
    mats, sides, low = partial_grams(got, mem_count, tile_count, local_members)
    own_mat = mats[1]
    own_vec = sides[0, 1]
    diag_mask = jnp.eye(members, dtype=jnp.bool_)
    from_prev = ring_shift(low[0], axis, 1)
    from_prev_side = ring_shift(sides[:, 0], axis, 1)
    from_next = ring_shift(low[1], axis, -1)
    from_next_side = ring_shift(sides[:, 2], axis, -1)
    from_prev = jnp.where(diag_mask, from_prev_side[1][None, :], from_prev.astype(jnp.float32))
    from_next = jnp.where(diag_mask, from_next_side[1][None, :], from_next.astype(jnp.float32))
    gram_mat = own_mat + from_prev + from_next
    gram_vec = own_vec + from_prev_side[0] + from_next_side[0]
    transform_mat = transform(gram_mat, gram_vec)

    mixed = lax.dot_general(
        transform_mat, deviation, (((0,), (0,)), ((), ())), preferred_element_type=jnp.float32
    )
    updated = (state_mean[None, :] + mixed).astype(jnp.bfloat16)
    chunks = updated.reshape(mem_count, local_members, cells)
    me = lax.axis_index("mem")
    pieces = []
    for shift in range(mem_count):
        piece = lax.dynamic_index_in_dim(chunks, (me + shift) % mem_count, 0, keepdims=False)
        if shift:
            pairs = [(i, (i + shift) % mem_count) for i in range(mem_count)]
            piece = lax.ppermute(piece, "mem", pairs)
        pieces.append(piece)
    by_shift = jnp.stack(pieces)
    back = jnp.take(by_shift, (me - jnp.arange(mem_count)) % mem_count, axis=0)
    return back.transpose(1, 0, 2).reshape(local_members, mem_count, 1, cells)


def solution(mesh):
    return jax.shard_map(
        per_device,
        mesh=mesh,
        in_specs=(
            P("mem", None, "tile", None),
            P("mem", "tile"),
            P("tile"),
            P("tile"),
            P("tile", None),
            P("tile"),
        ),
        out_specs=P("mem", None, "tile", None),
        check_vma=False,
    )
```

```python
import functools
import math

import jax
import jax.numpy as jnp
from jax import lax
from jax.experimental import pallas as pl
from jax.sharding import PartitionSpec as P

PATCH_CELLS = 128
OBS_PATCH = 1024
ITERS = 4
HIGHEST = lax.Precision.HIGHEST
NEWTON = lax.Precision.HIGH


def ring_shift(block, axis, step):
    count = 1
    for name in axis:
        count *= lax.axis_size(name)
    pairs = [(i, (i + step) % count) for i in range(count)]
    return lax.ppermute(block, axis, pairs)


def localize(position, offset):
    distance = (offset * PATCH_CELLS + position + 0.5 - 0.5 * PATCH_CELLS) / PATCH_CELLS
    return jnp.exp(-2.0 * distance * distance)


def obs_weight(var_row, shifted_row):
    is_live = shifted_row.astype(jnp.float32) > 0.5
    safe_var = jnp.where(is_live, var_row.astype(jnp.float32), 1.0)
    return (jnp.where(is_live, 1.0 / safe_var, 0.0), shifted_row.astype(jnp.float32) - 1.0)


def block_terms(block, members, offset):
    centred = block[:members]
    innovation = block[members]
    weight, position = obs_weight(block[members + 1], block[members + 2])
    scale = weight * localize(position, offset)
    weighted = (centred.astype(jnp.float32) * scale[None, :]).astype(jnp.bfloat16)
    gram_mat = lax.dot_general(
        weighted, centred, (((1,), (1,)), ((), ())), preferred_element_type=jnp.float32
    )
    gram_vec = jnp.dot(weighted, innovation, preferred_element_type=jnp.float32)
    return gram_mat, gram_vec


def gram_kernel(x_ref, mat_ref, vec_ref, low_ref, *, local_members, mem_count, tiles_per_step):
    step = pl.program_id(0)

    @pl.when(step == 0)
    def _():
        mat_ref[...] = jnp.zeros_like(mat_ref)
        vec_ref[...] = jnp.zeros_like(vec_ref)

    members = local_members * mem_count
    block = x_ref[...]
    slots = block.shape[-1]
    values = jnp.concatenate(
        [block[:, j, :local_members, :].reshape(members, slots) for j in range(tiles_per_step)], 1
    ).astype(jnp.float32)
    info = jnp.concatenate(
        [block[0, j, local_members:local_members + 3, :] for j in range(tiles_per_step)], 1
    ).astype(jnp.float32)
    obs_mean = jnp.sum(values, 0, keepdims=True) / members
    centred = (values - obs_mean).astype(jnp.bfloat16)
    innovation = (info[0:1] - obs_mean).astype(jnp.bfloat16)
    is_live = info[2:3] > 0.5
    weight = jnp.where(is_live, 1.0 / jnp.where(is_live, info[1:2], 1.0), 0.0)
    position = info[2:3] - 1.0
    centred_f = centred.astype(jnp.float32)
    weighted = jnp.concatenate(
        [
            (centred_f * (weight * localize(position, offset))).astype(jnp.bfloat16)
            for offset in (-1.0, 0.0, 1.0)
        ],
        0,
    )
    mat_ref[...] += lax.dot_general(
        weighted, centred, (((1,), (1,)), ((), ())), preferred_element_type=jnp.float32
    )
    innov_rows = jnp.broadcast_to(innovation, (8, innovation.shape[1]))
    vec_ref[...] += lax.dot_general(
        innov_rows, weighted, (((1,), (1,)), ((), ())), preferred_element_type=jnp.float32
    )

    @pl.when(step == pl.num_programs(0) - 1)
    def _():
        diag_mask = (
            lax.broadcasted_iota(jnp.int32, (members, members), 0)
            == lax.broadcasted_iota(jnp.int32, (members, members), 1)
        )
        for index, part in enumerate((0, 2)):
            mat = mat_ref[part * members:(part + 1) * members, :]
            low_ref[index, :members, :] = mat.astype(jnp.bfloat16)
            diag = jnp.sum(jnp.where(diag_mask, mat, 0.0), 0, keepdims=True)
            vec = vec_ref[0:1, part * members:(part + 1) * members]
            side = []
            for value in (vec, diag):
                high = value.astype(jnp.bfloat16).astype(jnp.float32)
                side += [high, (value - high).astype(jnp.bfloat16).astype(jnp.float32)]
            side.append(jnp.zeros((12, members), jnp.float32))
            low_ref[index, members:, :] = jnp.concatenate(side, 0).astype(jnp.bfloat16)


def partial_grams(received, mem_count, tile_count, local_members):
    rows, slots = received.shape[1], received.shape[2]
    members = local_members * mem_count
    tiles_per_step = 4
    x = received.reshape(mem_count, tile_count, rows, slots)
    kernel = functools.partial(
        gram_kernel, local_members=local_members, mem_count=mem_count, tiles_per_step=tiles_per_step
    )
    mat, vec, low = pl.pallas_call(
        kernel,
        grid=(tile_count // tiles_per_step,),
        in_specs=[pl.BlockSpec((mem_count, tiles_per_step, rows, slots), lambda t: (0, t, 0, 0))],
        out_specs=[
            pl.BlockSpec((3 * members, members), lambda t: (0, 0)),
            pl.BlockSpec((8, 3 * members), lambda t: (0, 0)),
            pl.BlockSpec((2, members + 16, members), lambda t: (0, 0, 0)),
        ],
        out_shape=[
            jax.ShapeDtypeStruct((3 * members, members), jnp.float32),
            jax.ShapeDtypeStruct((8, 3 * members), jnp.float32),
            jax.ShapeDtypeStruct((2, members + 16, members), jnp.bfloat16),
        ],
    )(x)
    return mat.reshape(3, members, members), vec[:2].reshape(2, 3, members), low


def inverse_root(gram_mat):
    mat_size = gram_mat.shape[0]
    identity = jnp.eye(mat_size, dtype=jnp.float32)
    norm_scale = jnp.sqrt(jnp.sum(gram_mat * gram_mat))
    root_up = gram_mat / norm_scale
    root_down = None
    for sweep_index in range(ITERS):
        if root_down is None:
            product = root_up
        else:
            product = jnp.dot(root_down, root_up, precision=NEWTON)
        middle = 1.5 * identity - 0.5 * product
        if sweep_index + 1 < ITERS:
            root_up = jnp.dot(root_up, middle, precision=NEWTON)
        root_down = middle if root_down is None else jnp.dot(middle, root_down, precision=NEWTON)
    return root_down / jnp.sqrt(norm_scale)


def transform(gram_mat, gram_vec):
    mat_size = gram_mat.shape[0]
    identity = jnp.eye(mat_size, dtype=jnp.float32)
    inv_root = inverse_root(gram_mat + (mat_size - 1.0) * identity)
    inner_w = jnp.dot(inv_root, gram_vec, precision=NEWTON)
    mean_w = jnp.dot(inv_root, inner_w, precision=NEWTON)
    return (math.sqrt(mat_size - 1.0) * inv_root + mean_w[:, None]).astype(jnp.bfloat16)


def rank_in_patch(target, patches):
    rows = target.shape[0]
    block = 128
    blocks = rows // block
    onehot = (target[:, None] == jnp.arange(patches, dtype=jnp.int32)[None, :]).astype(jnp.bfloat16)
    onehot = onehot.reshape(blocks, block, patches)
    lower = (jnp.arange(block)[:, None] >= jnp.arange(block)[None, :]).astype(jnp.bfloat16)
    within = jnp.einsum("ij,bjp->bip", lower, onehot, preferred_element_type=jnp.float32)
    totals = jnp.sum(onehot.astype(jnp.float32), 1)
    earlier = (jnp.arange(blocks)[:, None] > jnp.arange(blocks)[None, :]).astype(jnp.float32)
    before = jnp.dot(earlier, totals, precision=HIGHEST)
    count = jnp.sum((within + before[:, None, :]) * onehot.astype(jnp.float32), 2)
    return count.reshape(rows).astype(jnp.int32) - 1


def per_device(background, evolved, obs_value, obs_var, obs_patch, obs_pos):
    mem_count = lax.axis_size("mem")
    tile_count = lax.axis_size("tile")
    patches = mem_count * tile_count
    local_members = evolved.shape[0]
    members = local_members * mem_count
    slot_count = 2 * OBS_PATCH
    capacity = slot_count // tile_count
    cells = background.shape[3]

    states = lax.all_to_all(background, "mem", split_axis=1, concat_axis=0, tiled=True)
    flat_states = states.reshape(members, cells)
    state_sum = jnp.sum(flat_states.astype(jnp.float32), 0)
    state_mean = state_sum / members
    deviation = (flat_states.astype(jnp.float32) - state_mean[None, :]).astype(jnp.bfloat16)

    target = obs_patch[:, 0]
    slot_rank = rank_in_patch(target, patches)
    slot_place = target * capacity + slot_rank
    rows = jnp.concatenate(
        [evolved, jnp.stack([obs_value, obs_var, (obs_pos + 1).astype(jnp.bfloat16)])], 0
    )
    send = jnp.zeros((rows.shape[0], patches * capacity), jnp.bfloat16).at[:, slot_place].set(rows)
    send = send.reshape(rows.shape[0], patches, capacity).transpose(1, 0, 2)
    got = lax.all_to_all(send, ("mem", "tile"), split_axis=0, concat_axis=0, tiled=True)
    axis = ("mem", "tile")
    mats, sides, low = partial_grams(got, mem_count, tile_count, local_members)
    own_mat = mats[1]
    own_vec = sides[0, 1]
    diag_mask = jnp.eye(members, dtype=jnp.bool_)
    from_prev = ring_shift(low[0], axis, 1).astype(jnp.float32)
    from_next = ring_shift(low[1], axis, -1).astype(jnp.float32)
    prev_side = from_prev[members:members + 4]
    next_side = from_next[members:members + 4]
    from_prev_vec = prev_side[0] + prev_side[1]
    from_next_vec = next_side[0] + next_side[1]
    from_prev = jnp.where(diag_mask, (prev_side[2] + prev_side[3])[None, :], from_prev[:members])
    from_next = jnp.where(diag_mask, (next_side[2] + next_side[3])[None, :], from_next[:members])
    gram_mat = own_mat + from_prev + from_next
    gram_vec = own_vec + from_prev_vec + from_next_vec
    transform_mat = transform(gram_mat, gram_vec)

    mixed = lax.dot_general(
        transform_mat, deviation, (((0,), (0,)), ((), ())), preferred_element_type=jnp.float32
    )
    updated = (state_mean[None, :] + mixed).astype(jnp.bfloat16)
    chunks = updated.reshape(mem_count, local_members, cells)
    me = lax.axis_index("mem")
    pieces = []
    for shift in range(mem_count):
        piece = lax.dynamic_index_in_dim(chunks, (me + shift) % mem_count, 0, keepdims=False)
        if shift:
            pairs = [(i, (i + shift) % mem_count) for i in range(mem_count)]
            piece = lax.ppermute(piece, "mem", pairs)
        pieces.append(piece)
    by_shift = jnp.stack(pieces)
    back = jnp.take(by_shift, (me - jnp.arange(mem_count)) % mem_count, axis=0)
    return back.transpose(1, 0, 2).reshape(local_members, mem_count, 1, cells)


def solution(mesh):
    return jax.shard_map(
        per_device,
        mesh=mesh,
        in_specs=(
            P("mem", None, "tile", None),
            P("mem", "tile"),
            P("tile"),
            P("tile"),
            P("tile", None),
            P("tile"),
        ),
        out_specs=P("mem", None, "tile", None),
        check_vma=False,
    )
```

```python
import functools
import math

import jax
import jax.numpy as jnp
from jax import lax
from jax.experimental import pallas as pl
from jax.sharding import PartitionSpec as P

PATCH_CELLS = 128
OBS_PATCH = 1024
ITERS = 4
HIGHEST = lax.Precision.HIGHEST
NEWTON = lax.Precision.HIGH


def ring_shift(block, axis, step):
    count = 1
    for name in axis:
        count *= lax.axis_size(name)
    pairs = [(i, (i + step) % count) for i in range(count)]
    return lax.ppermute(block, axis, pairs)


def localize(position, offset):
    distance = (offset * PATCH_CELLS + position + 0.5 - 0.5 * PATCH_CELLS) / PATCH_CELLS
    return jnp.exp(-2.0 * distance * distance)


def obs_weight(var_row, shifted_row):
    is_live = shifted_row.astype(jnp.float32) > 0.5
    safe_var = jnp.where(is_live, var_row.astype(jnp.float32), 1.0)
    return (jnp.where(is_live, 1.0 / safe_var, 0.0), shifted_row.astype(jnp.float32) - 1.0)


def block_terms(block, members, offset):
    centred = block[:members]
    innovation = block[members]
    weight, position = obs_weight(block[members + 1], block[members + 2])
    scale = weight * localize(position, offset)
    weighted = (centred.astype(jnp.float32) * scale[None, :]).astype(jnp.bfloat16)
    gram_mat = lax.dot_general(
        weighted, centred, (((1,), (1,)), ((), ())), preferred_element_type=jnp.float32
    )
    gram_vec = jnp.dot(weighted, innovation, preferred_element_type=jnp.float32)
    return gram_mat, gram_vec


def gram_kernel(x_ref, mat_ref, vec_ref, low_ref, *, local_members, mem_count, tiles_per_step):
    step = pl.program_id(0)

    @pl.when(step == 0)
    def _():
        mat_ref[...] = jnp.zeros_like(mat_ref)
        vec_ref[...] = jnp.zeros_like(vec_ref)

    members = local_members * mem_count
    block = x_ref[...]
    slots = block.shape[-1]
    values = jnp.concatenate(
        [block[:, j, :local_members, :].reshape(members, slots) for j in range(tiles_per_step)], 1
    ).astype(jnp.float32)
    info = jnp.concatenate(
        [block[0, j, local_members:local_members + 3, :] for j in range(tiles_per_step)], 1
    ).astype(jnp.float32)
    obs_mean = jnp.sum(values, 0, keepdims=True) / members
    centred = (values - obs_mean).astype(jnp.bfloat16)
    innovation = (info[0:1] - obs_mean).astype(jnp.bfloat16)
    is_live = info[2:3] > 0.5
    weight = jnp.where(is_live, 1.0 / jnp.where(is_live, info[1:2], 1.0), 0.0)
    position = info[2:3] - 1.0
    centred_f = centred.astype(jnp.float32)
    weighted = jnp.concatenate(
        [
            (centred_f * (weight * localize(position, offset))).astype(jnp.bfloat16)
            for offset in (-1.0, 0.0, 1.0)
        ],
        0,
    )
    mat_ref[...] += lax.dot_general(
        weighted, centred, (((1,), (1,)), ((), ())), preferred_element_type=jnp.float32
    )
    innov_rows = jnp.broadcast_to(innovation, (8, innovation.shape[1]))
    vec_ref[...] += lax.dot_general(
        innov_rows, weighted, (((1,), (1,)), ((), ())), preferred_element_type=jnp.float32
    )

    @pl.when(step == pl.num_programs(0) - 1)
    def _():
        diag_mask = (
            lax.broadcasted_iota(jnp.int32, (members, members), 0)
            == lax.broadcasted_iota(jnp.int32, (members, members), 1)
        )
        for index, part in enumerate((0, 2)):
            mat = mat_ref[part * members:(part + 1) * members, :]
            low_ref[index, :members, :] = mat.astype(jnp.bfloat16)
            diag = jnp.sum(jnp.where(diag_mask, mat, 0.0), 0, keepdims=True)
            vec = vec_ref[0:1, part * members:(part + 1) * members]
            side = []
            for value in (vec, diag):
                high = value.astype(jnp.bfloat16).astype(jnp.float32)
                side += [high, (value - high).astype(jnp.bfloat16).astype(jnp.float32)]
            side.append(jnp.zeros((12, members), jnp.float32))
            low_ref[index, members:, :] = jnp.concatenate(side, 0).astype(jnp.bfloat16)


def partial_grams(received, mem_count, tile_count, local_members):
    rows, slots = received.shape[1], received.shape[2]
    members = local_members * mem_count
    tiles_per_step = 4
    x = received.reshape(mem_count, tile_count, rows, slots)
    kernel = functools.partial(
        gram_kernel, local_members=local_members, mem_count=mem_count, tiles_per_step=tiles_per_step
    )
    mat, vec, low = pl.pallas_call(
        kernel,
        grid=(tile_count // tiles_per_step,),
        in_specs=[pl.BlockSpec((mem_count, tiles_per_step, rows, slots), lambda t: (0, t, 0, 0))],
        out_specs=[
            pl.BlockSpec((3 * members, members), lambda t: (0, 0)),
            pl.BlockSpec((8, 3 * members), lambda t: (0, 0)),
            pl.BlockSpec((2, members + 16, members), lambda t: (0, 0, 0)),
        ],
        out_shape=[
            jax.ShapeDtypeStruct((3 * members, members), jnp.float32),
            jax.ShapeDtypeStruct((8, 3 * members), jnp.float32),
            jax.ShapeDtypeStruct((2, members + 16, members), jnp.bfloat16),
        ],
    )(x)
    return mat.reshape(3, members, members), vec[:2].reshape(2, 3, members), low


def inverse_root(gram_mat):
    mat_size = gram_mat.shape[0]
    identity = jnp.eye(mat_size, dtype=jnp.float32)
    norm_scale = jnp.sqrt(jnp.sum(gram_mat * gram_mat))
    root_up = gram_mat / norm_scale
    root_down = None
    for sweep_index in range(ITERS):
        if root_down is None:
            product = root_up
        else:
            product = jnp.dot(root_down, root_up, precision=NEWTON)
        middle = 1.5 * identity - 0.5 * product
        if sweep_index + 1 < ITERS:
            root_up = jnp.dot(root_up, middle, precision=NEWTON)
        root_down = middle if root_down is None else jnp.dot(middle, root_down, precision=NEWTON)
    return root_down / jnp.sqrt(norm_scale)


def transform(gram_mat, gram_vec):
    mat_size = gram_mat.shape[0]
    identity = jnp.eye(mat_size, dtype=jnp.float32)
    inv_root = inverse_root(gram_mat + (mat_size - 1.0) * identity)
    inner_w = jnp.dot(inv_root, gram_vec, precision=NEWTON)
    mean_w = jnp.dot(inv_root, inner_w, precision=NEWTON)
    return (math.sqrt(mat_size - 1.0) * inv_root + mean_w[:, None]).astype(jnp.bfloat16)


def rank_in_patch(target, patches):
    rows = target.shape[0]
    block = 128
    blocks = rows // block
    onehot = (target[:, None] == jnp.arange(patches, dtype=jnp.int32)[None, :]).astype(jnp.bfloat16)
    onehot = onehot.reshape(blocks, block, patches)
    lower = (jnp.arange(block)[:, None] >= jnp.arange(block)[None, :]).astype(jnp.bfloat16)
    within = jnp.einsum("ij,bjp->bip", lower, onehot, preferred_element_type=jnp.float32)
    totals = jnp.sum(onehot.astype(jnp.float32), 1)
    earlier = (jnp.arange(blocks)[:, None] > jnp.arange(blocks)[None, :]).astype(jnp.float32)
    before = jnp.dot(earlier, totals, precision=HIGHEST)
    count = jnp.sum((within + before[:, None, :]) * onehot.astype(jnp.float32), 2)
    return count.reshape(rows).astype(jnp.int32) - 1


def per_device(background, evolved, obs_value, obs_var, obs_patch, obs_pos):
    mem_count = lax.axis_size("mem")
    tile_count = lax.axis_size("tile")
    patches = mem_count * tile_count
    local_members = evolved.shape[0]
    members = local_members * mem_count
    slot_count = 2 * OBS_PATCH
    capacity = slot_count // tile_count
    cells = background.shape[3]

    states = lax.all_to_all(background, "mem", split_axis=1, concat_axis=0, tiled=True)
    flat_states = states.reshape(members, cells)
    state_sum = jnp.sum(flat_states.astype(jnp.float32), 0)
    state_mean = state_sum / members
    deviation = (flat_states.astype(jnp.float32) - state_mean[None, :]).astype(jnp.bfloat16)

    target = obs_patch[:, 0]
    slot_rank = rank_in_patch(target, patches)
    slot_place = target * capacity + slot_rank
    rows = jnp.concatenate(
        [evolved, jnp.stack([obs_value, obs_var, (obs_pos + 1).astype(jnp.bfloat16)])], 0
    )
    send = jnp.zeros((rows.shape[0], patches * capacity), jnp.bfloat16).at[:, slot_place].set(rows)
    send = send.reshape(rows.shape[0], patches, capacity).transpose(1, 0, 2)
    got = lax.all_to_all(send, ("mem", "tile"), split_axis=0, concat_axis=0, tiled=True)
    axis = ("mem", "tile")
    mats, sides, low = partial_grams(got, mem_count, tile_count, local_members)
    own_mat = mats[1]
    own_vec = sides[0, 1]
    diag_mask = jnp.eye(members, dtype=jnp.bool_)
    from_prev = ring_shift(low[0], axis, 1).astype(jnp.float32)
    from_next = ring_shift(low[1], axis, -1).astype(jnp.float32)
    prev_side = from_prev[members:members + 4]
    next_side = from_next[members:members + 4]
    from_prev_vec = prev_side[0] + prev_side[1]
    from_next_vec = next_side[0] + next_side[1]
    from_prev = jnp.where(diag_mask, (prev_side[2] + prev_side[3])[None, :], from_prev[:members])
    from_next = jnp.where(diag_mask, (next_side[2] + next_side[3])[None, :], from_next[:members])
    gram_mat = own_mat + from_prev + from_next
    gram_vec = own_vec + from_prev_vec + from_next_vec
    transform_mat = transform(gram_mat, gram_vec)

    mixed = lax.dot_general(
        transform_mat, deviation, (((0,), (0,)), ((), ())), preferred_element_type=jnp.float32
    )
    updated = (state_mean[None, :] + mixed).astype(jnp.bfloat16)
    chunks = updated.reshape(mem_count, local_members, cells)
    me = lax.axis_index("mem")
    pieces = []
    for shift in range(mem_count):
        piece = lax.dynamic_index_in_dim(chunks, (me + shift) % mem_count, 0, keepdims=False)
        if shift:
            pairs = [(i, (i + shift) % mem_count) for i in range(mem_count)]
            piece = lax.ppermute(piece, "mem", pairs)
        pieces.append(piece)
    by_shift = jnp.stack(pieces[::-1], 1)
    back = jnp.roll(by_shift, me + 1, axis=1)
    return back.reshape(local_members, mem_count, 1, cells)


def solution(mesh):
    return jax.shard_map(
        per_device,
        mesh=mesh,
        in_specs=(
            P("mem", None, "tile", None),
            P("mem", "tile"),
            P("tile"),
            P("tile"),
            P("tile", None),
            P("tile"),
        ),
        out_specs=P("mem", None, "tile", None),
        check_vma=False,
    )
```

```python
import functools
import math

import jax
import jax.numpy as jnp
from jax import lax
from jax.experimental import pallas as pl
from jax.experimental.pallas import tpu as pltpu
from jax.sharding import PartitionSpec as P

PATCH_CELLS = 128
OBS_PATCH = 1024
ITERS = 4
HIGHEST = lax.Precision.HIGHEST
NEWTON = lax.Precision.HIGH


def ring_shift(block, axis, step):
    count = 1
    for name in axis:
        count *= lax.axis_size(name)
    pairs = [(i, (i + step) % count) for i in range(count)]
    return lax.ppermute(block, axis, pairs)


def localize(position, offset):
    distance = (offset * PATCH_CELLS + position + 0.5 - 0.5 * PATCH_CELLS) / PATCH_CELLS
    return jnp.exp(-2.0 * distance * distance)


def obs_weight(var_row, shifted_row):
    is_live = shifted_row.astype(jnp.float32) > 0.5
    safe_var = jnp.where(is_live, var_row.astype(jnp.float32), 1.0)
    return (jnp.where(is_live, 1.0 / safe_var, 0.0), shifted_row.astype(jnp.float32) - 1.0)


def block_terms(block, members, offset):
    centred = block[:members]
    innovation = block[members]
    weight, position = obs_weight(block[members + 1], block[members + 2])
    scale = weight * localize(position, offset)
    weighted = (centred.astype(jnp.float32) * scale[None, :]).astype(jnp.bfloat16)
    gram_mat = lax.dot_general(
        weighted, centred, (((1,), (1,)), ((), ())), preferred_element_type=jnp.float32
    )
    gram_vec = jnp.dot(weighted, innovation, preferred_element_type=jnp.float32)
    return gram_mat, gram_vec


def gram_kernel(x_ref, mat_ref, vec_ref, low_ref, col_ref, *, local_members, mem_count, tiles_per_step):
    step = pl.program_id(0)

    @pl.when(step == 0)
    def _():
        mat_ref[...] = jnp.zeros_like(mat_ref)
        col_ref[...] = jnp.zeros_like(col_ref)

    members = local_members * mem_count
    block = x_ref[...]
    slots = block.shape[-1]
    values = jnp.concatenate(
        [block[:, j, :local_members, :].reshape(members, slots) for j in range(tiles_per_step)], 1
    ).astype(jnp.float32)
    info = jnp.concatenate(
        [block[0, j, local_members:local_members + 3, :] for j in range(tiles_per_step)], 1
    ).astype(jnp.float32)
    obs_mean = jnp.sum(values, 0, keepdims=True) / members
    centred = (values - obs_mean).astype(jnp.bfloat16)
    innovation = (info[0:1] - obs_mean).astype(jnp.bfloat16)
    is_live = info[2:3] > 0.5
    weight = jnp.where(is_live, 1.0 / jnp.where(is_live, info[1:2], 1.0), 0.0)
    position = info[2:3] - 1.0
    centred_f = centred.astype(jnp.float32)
    weighted = jnp.concatenate(
        [
            (centred_f * (weight * localize(position, offset))).astype(jnp.bfloat16)
            for offset in (-1.0, 0.0, 1.0)
        ],
        0,
    )
    mat_ref[...] += lax.dot_general(
        weighted, centred, (((1,), (1,)), ((), ())), preferred_element_type=jnp.float32
    )
    innov_rows = jnp.broadcast_to(innovation, (128, innovation.shape[1]))
    col_ref[...] += lax.dot_general(
        weighted, innov_rows, (((1,), (1,)), ((), ())), preferred_element_type=jnp.float32
    )

    @pl.when(step == pl.num_programs(0) - 1)
    def _():
        for part in range(3):
            cols = col_ref[part * members:(part + 1) * members, :]
            vec_ref[:, part * members:(part + 1) * members] = jnp.transpose(cols)[:8]

    @pl.when(step == pl.num_programs(0) - 1)
    def _():
        diag_mask = (
            lax.broadcasted_iota(jnp.int32, (members, members), 0)
            == lax.broadcasted_iota(jnp.int32, (members, members), 1)
        )
        for index, part in enumerate((0, 2)):
            mat = mat_ref[part * members:(part + 1) * members, :]
            low_ref[index, :members, :] = mat.astype(jnp.bfloat16)
            diag = jnp.sum(jnp.where(diag_mask, mat, 0.0), 0, keepdims=True)
            vec = vec_ref[0:1, part * members:(part + 1) * members]
            side = []
            for value in (vec, diag):
                high = value.astype(jnp.bfloat16).astype(jnp.float32)
                side += [high, (value - high).astype(jnp.bfloat16).astype(jnp.float32)]
            side.append(jnp.zeros((12, members), jnp.float32))
            low_ref[index, members:, :] = jnp.concatenate(side, 0).astype(jnp.bfloat16)


def partial_grams(received, mem_count, tile_count, local_members):
    rows, slots = received.shape[1], received.shape[2]
    members = local_members * mem_count
    tiles_per_step = 4
    x = received.reshape(mem_count, tile_count, rows, slots)
    kernel = functools.partial(
        gram_kernel, local_members=local_members, mem_count=mem_count, tiles_per_step=tiles_per_step
    )
    mat, vec, low = pl.pallas_call(
        kernel,
        grid=(tile_count // tiles_per_step,),
        in_specs=[pl.BlockSpec((mem_count, tiles_per_step, rows, slots), lambda t: (0, t, 0, 0))],
        out_specs=[
            pl.BlockSpec((3 * members, members), lambda t: (0, 0)),
            pl.BlockSpec((8, 3 * members), lambda t: (0, 0)),
            pl.BlockSpec((2, members + 16, members), lambda t: (0, 0, 0)),
        ],
        out_shape=[
            jax.ShapeDtypeStruct((3 * members, members), jnp.float32),
            jax.ShapeDtypeStruct((8, 3 * members), jnp.float32),
            jax.ShapeDtypeStruct((2, members + 16, members), jnp.bfloat16),
        ],
        scratch_shapes=[pltpu.VMEM((3 * members, 128), jnp.float32)],
    )(x)
    return mat.reshape(3, members, members), vec[:2].reshape(2, 3, members), low


def inverse_root(gram_mat):
    mat_size = gram_mat.shape[0]
    identity = jnp.eye(mat_size, dtype=jnp.float32)
    norm_scale = jnp.sqrt(jnp.sum(gram_mat * gram_mat))
    root_up = gram_mat / norm_scale
    root_down = None
    for sweep_index in range(ITERS):
        if root_down is None:
            product = root_up
        else:
            product = jnp.dot(root_down, root_up, precision=NEWTON)
        middle = 1.5 * identity - 0.5 * product
        if sweep_index + 1 < ITERS:
            root_up = jnp.dot(root_up, middle, precision=NEWTON)
        root_down = middle if root_down is None else jnp.dot(middle, root_down, precision=NEWTON)
    return root_down / jnp.sqrt(norm_scale)


def transform(gram_mat, gram_vec):
    mat_size = gram_mat.shape[0]
    identity = jnp.eye(mat_size, dtype=jnp.float32)
    inv_root = inverse_root(gram_mat + (mat_size - 1.0) * identity)
    inner_w = jnp.dot(inv_root, gram_vec, precision=NEWTON)
    mean_w = jnp.dot(inv_root, inner_w, precision=NEWTON)
    return (math.sqrt(mat_size - 1.0) * inv_root + mean_w[:, None]).astype(jnp.bfloat16)


def rank_in_patch(target, patches):
    rows = target.shape[0]
    block = 128
    blocks = rows // block
    onehot = (target[:, None] == jnp.arange(patches, dtype=jnp.int32)[None, :]).astype(jnp.bfloat16)
    onehot = onehot.reshape(blocks, block, patches)
    lower = (jnp.arange(block)[:, None] >= jnp.arange(block)[None, :]).astype(jnp.bfloat16)
    within = jnp.einsum("ij,bjp->bip", lower, onehot, preferred_element_type=jnp.float32)
    totals = jnp.sum(onehot.astype(jnp.float32), 1)
    earlier = (jnp.arange(blocks)[:, None] > jnp.arange(blocks)[None, :]).astype(jnp.float32)
    before = jnp.dot(earlier, totals, precision=HIGHEST)
    count = jnp.sum((within + before[:, None, :]) * onehot.astype(jnp.float32), 2)
    return count.reshape(rows).astype(jnp.int32) - 1


def per_device(background, evolved, obs_value, obs_var, obs_patch, obs_pos):
    mem_count = lax.axis_size("mem")
    tile_count = lax.axis_size("tile")
    patches = mem_count * tile_count
    local_members = evolved.shape[0]
    members = local_members * mem_count
    slot_count = 2 * OBS_PATCH
    capacity = slot_count // tile_count
    cells = background.shape[3]

    states = lax.all_to_all(background, "mem", split_axis=1, concat_axis=0, tiled=True)
    flat_states = states.reshape(members, cells)
    state_sum = jnp.sum(flat_states.astype(jnp.float32), 0)
    state_mean = state_sum / members
    deviation = (flat_states.astype(jnp.float32) - state_mean[None, :]).astype(jnp.bfloat16)

    target = obs_patch[:, 0]
    slot_rank = rank_in_patch(target, patches)
    slot_place = target * capacity + slot_rank
    rows = jnp.concatenate(
        [evolved, jnp.stack([obs_value, obs_var, (obs_pos + 1).astype(jnp.bfloat16)])], 0
    )
    send = jnp.zeros((rows.shape[0], patches * capacity), jnp.bfloat16).at[:, slot_place].set(rows)
    send = send.reshape(rows.shape[0], patches, capacity).transpose(1, 0, 2)
    got = lax.all_to_all(send, ("mem", "tile"), split_axis=0, concat_axis=0, tiled=True)
    axis = ("mem", "tile")
    mats, sides, low = partial_grams(got, mem_count, tile_count, local_members)
    own_mat = mats[1]
    own_vec = sides[0, 1]
    diag_mask = jnp.eye(members, dtype=jnp.bool_)
    from_prev = ring_shift(low[0], axis, 1).astype(jnp.float32)
    from_next = ring_shift(low[1], axis, -1).astype(jnp.float32)
    prev_side = from_prev[members:members + 4]
    next_side = from_next[members:members + 4]
    from_prev_vec = prev_side[0] + prev_side[1]
    from_next_vec = next_side[0] + next_side[1]
    from_prev = jnp.where(diag_mask, (prev_side[2] + prev_side[3])[None, :], from_prev[:members])
    from_next = jnp.where(diag_mask, (next_side[2] + next_side[3])[None, :], from_next[:members])
    gram_mat = own_mat + from_prev + from_next
    gram_vec = own_vec + from_prev_vec + from_next_vec
    transform_mat = transform(gram_mat, gram_vec)

    mixed = lax.dot_general(
        transform_mat, deviation, (((0,), (0,)), ((), ())), preferred_element_type=jnp.float32
    )
    updated = (state_mean[None, :] + mixed).astype(jnp.bfloat16)
    chunks = updated.reshape(mem_count, local_members, cells)
    me = lax.axis_index("mem")
    pieces = []
    for shift in range(mem_count):
        piece = lax.dynamic_index_in_dim(chunks, (me + shift) % mem_count, 0, keepdims=False)
        if shift:
            pairs = [(i, (i + shift) % mem_count) for i in range(mem_count)]
            piece = lax.ppermute(piece, "mem", pairs)
        pieces.append(piece)
    by_shift = jnp.stack(pieces)
    back = jnp.take(by_shift, (me - jnp.arange(mem_count)) % mem_count, axis=0)
    return back.transpose(1, 0, 2).reshape(local_members, mem_count, 1, cells)


def solution(mesh):
    return jax.shard_map(
        per_device,
        mesh=mesh,
        in_specs=(
            P("mem", None, "tile", None),
            P("mem", "tile"),
            P("tile"),
            P("tile"),
            P("tile", None),
            P("tile"),
        ),
        out_specs=P("mem", None, "tile", None),
        check_vma=False,
    )
```
